512 devices in a mesh: kx: 16 (over x_lo, y, core), ky: 32 (over z, x_hi).
Axes of the slice: x: 4 (x_hi: 2, x_lo: 2; x = x_hi * 2 + x_lo), y: 4, z: 16, core: 2. Of those that a mesh axis runs over, the one named last changes fastest.
Arguments:
- packed_state_matrix: float32 [16, 512, 4096], P(None, 'kx', 'ky'), may hold values from -1 to 1, as said below
- energies: float32 [4, 512, 4096], P(None, 'kx', 'ky'), may hold values from -2.4 to 2.4
- dipole_x: float32 [12, 512, 4096], P(None, 'kx', 'ky'), may hold values from -2.5 to 2.5
- dipole_y: float32 [12, 512, 4096], P(None, 'kx', 'ky'), may hold values from -2.5 to 2.5
- interaction: float32 [512, 4096], P('ky'), may hold values from 0.3 to 5, as said below
- driving_field: float32 [2], replicated, may hold values from 0.3 to 1
Outputs:
- section_slope: float32 [16, 512, 4096], P(None, 'kx', 'ky')
- field_next: float32 [2], replicated
The draws below stay inside these ranges and needn't reach their ends.
Inputs may be any that keep to these rules, and one draw needn't show every extreme that they name: `packed_state_matrix`: components 0 to 3 lie in 0 to 1. interaction at (p, q) equals interaction at ((-p) mod 512, q) and at (p, (-q) mod 4096).
All inputs are finite; a program needn't handle non-finite values.
Results may differ from the reference program's by a relative error of at most 0.000054.
Values sent between devices are 32-bit elements; how exact they have to be, the bound alone decides.
No kernel may reach another device: no remote copies, remote signals or barrier semaphores. Data moves between devices by JAX's collectives and lax.ppermute only.
A program may use at most 64 MiB of HBM per device.

```python
import jax
import jax.numpy as jnp
from jax import lax

NKX = 512
NKY = 4096


def band_fields(key):
    disorder_seed = jax.random.fold_in(key, 101)
    row_key = jax.random.fold_in(key, 102)
    column_key = jax.random.fold_in(key, 103)
    row_place = jnp.arange(NKX, dtype=jnp.float32) / NKX
    column_place = jnp.arange(NKY, dtype=jnp.float32) / NKY
    roughness = jnp.clip(0.4 * jax.random.normal(disorder_seed, (4, NKX, NKY), jnp.float32), -0.8, 0.8)
    row_exponent = 0.5 * row_place + 0.5 * jax.random.uniform(row_key, (NKX,), jnp.float32)
    second_power_order = 0.5 * column_place + 0.5 * jax.random.uniform(column_key, (NKY,), jnp.float32)
    offsets = jnp.array([-1.6, -1.0, 1.0, 1.6], jnp.float32)
    energies = offsets[:, None, None] + roughness
    shifted = 0.5 * (jnp.roll(energies, 1, axis=1) + jnp.roll(energies, 1, axis=2))
    occupied = jax.nn.sigmoid(-2.0 * shifted)
    weight_grid = jnp.power(10.0, row_exponent[:, None] + second_power_order[None, :] - 2.0)
    return (energies, occupied * weight_grid[None])


def draw_packed_state_matrix(key, part):
    energies, populations = band_fields(key)
    coherence_key = jax.random.fold_in(key, 104)
    coherences = jnp.clip(0.25 * jax.random.normal(coherence_key, (12, NKX, NKY), jnp.float32), -1.0, 1.0)
    return jnp.concatenate([populations, coherences])


def draw_energies(key, part):
    energies, populations = band_fields(key)
    return energies


def mirror(values, axis_direction):
    return jnp.roll(jnp.flip(values, axis_direction), 1, axis_direction)


def draw_interaction(key, part):
    raw_key = jax.random.fold_in(key, 105)
    unscaled_values = jax.random.uniform(raw_key, (NKX, NKY), jnp.float32, 0.4, 4.0)
    return 0.25 * (unscaled_values + mirror(unscaled_values, 0) + mirror(unscaled_values, 1) + mirror(mirror(unscaled_values, 0), 1))


def steps_of(stream_key, dims, split, smallest, high):
    level, own = 1.0, jax.random.fold_in(stream_key, 6)
    for axis_at, parts in split:
        steps = jnp.exp(jax.random.uniform(jax.random.fold_in(own, axis_at), (parts,), jnp.float32, smallest / len(split), high / len(split)))
        level = level * jnp.repeat(steps, dims[axis_at] // parts).reshape([-1 if axis == axis_at else 1 for axis in range(len(dims))])
    return level


def centred(stream_key, dims, deviation, most, split=(), kind=jnp.bfloat16):
    values = deviation * jax.random.normal(stream_key, dims, jnp.float32)
    if split:
        values = values * steps_of(stream_key, dims, split, -0.22, 0.18)
    return jnp.clip(values, -most, most).astype(kind)


def setup_inputs(seed: int = 0) -> dict:
    keys = jax.random.split(jax.random.key(seed), 7)
    packed_state_matrix = draw_packed_state_matrix(jax.random.fold_in(keys[6], 71), 0)
    energies = draw_energies(jax.random.fold_in(keys[6], 71), 0)
    dipole_x = centred(keys[2], (12, NKX, NKY), 0.3, 2.5, ((1, 16), (2, 32)), jnp.float32)
    dipole_y = centred(keys[3], (12, NKX, NKY), 0.3, 2.5, ((1, 16), (2, 32)), jnp.float32)
    interaction = draw_interaction(jax.random.fold_in(keys[6], 71), 0)
    driving_field = jnp.clip(jax.random.uniform(keys[5], (2,), jnp.float32, 0.3, 1.0), 0.3, 1.0)
    return {"packed_state_matrix": packed_state_matrix, "energies": energies, "dipole_x": dipole_x, "dipole_y": dipole_y, "interaction": interaction, "driving_field": driving_field}


BAND_PAIRS = ((0, 1), (0, 2), (0, 3), (1, 2), (1, 3), (2, 3))
DEPHASING = 0.5
SHIELDING_LEVEL = 2.0
COUPLING = 40.0


def unpack(packed):
    real_entries = []
    imaginary_entries = []
    for band_one in range(4):
        real_entries.append([None, None, None, None])
        imaginary_entries.append([None, None, None, None])
    for band_one in range(4):
        real_entries[band_one][band_one] = packed[band_one]
    for number, band_pair in enumerate(BAND_PAIRS):
        upper_band, lower_band = band_pair
        real_entries[upper_band][lower_band] = packed[4 + number]
        real_entries[lower_band][upper_band] = packed[4 + number]
        imaginary_entries[upper_band][lower_band] = packed[10 + number]
        imaginary_entries[lower_band][upper_band] = -packed[10 + number]
    return real_entries, imaginary_entries


def product_sum(terms):
    summed = None
    for factor, left_value, right_value in terms:
        if left_value is None or right_value is None:
            continue
        product = factor * left_value * right_value
        summed = product if summed is None else summed + product
    return summed


def commutator(coupled, packed_state_matrix):
    coupled_real, coupled_imaginary = unpack(coupled)
    state_real, state_imaginary = unpack(packed_state_matrix)

    def element(row_band, column_band):
        real_terms = []
        imaginary_terms = []
        for middle in range(4):
            real_terms.append((1.0, coupled_real[row_band][middle], state_real[middle][column_band]))
            real_terms.append((-1.0, coupled_imaginary[row_band][middle], state_imaginary[middle][column_band]))
            real_terms.append((-1.0, state_real[row_band][middle], coupled_real[middle][column_band]))
            real_terms.append((1.0, state_imaginary[row_band][middle], coupled_imaginary[middle][column_band]))
            imaginary_terms.append((1.0, coupled_real[row_band][middle], state_imaginary[middle][column_band]))
            imaginary_terms.append((1.0, coupled_imaginary[row_band][middle], state_real[middle][column_band]))
            imaginary_terms.append((-1.0, state_real[row_band][middle], coupled_imaginary[middle][column_band]))
            imaginary_terms.append((-1.0, state_imaginary[row_band][middle], coupled_real[middle][column_band]))
        return product_sum(real_terms), product_sum(imaginary_terms)

    diagonal = []
    upper_real = []
    upper_imaginary = []
    for band_one in range(4):
        diagonal.append(element(band_one, band_one)[1])
    for upper_band, lower_band in BAND_PAIRS:
        real_value, imaginary_value = element(upper_band, lower_band)
        upper_real.append(imaginary_value)
        upper_imaginary.append(-real_value)
    return jnp.stack(diagonal + upper_real + upper_imaginary)


def slope_terms(packed_state_matrix, energies, self_energy, gradient_x, gradient_y, dipole_x, dipole_y, driving_field):
    field_x = driving_field[0]
    field_y = driving_field[1]
    coupled = jnp.concatenate([energies + self_energy[0:4], self_energy[4:16] + field_x * dipole_x + field_y * dipole_y])
    rotation = commutator(coupled, packed_state_matrix)
    drift = rotation + field_x * gradient_x + field_y * gradient_y
    return jnp.concatenate([drift[0:4], drift[4:16] - DEPHASING * packed_state_matrix[4:16]])


def grid_derivative(values, axis_direction):
    step_ahead = jnp.roll(values, -1, axis_direction)
    step_behind = jnp.roll(values, 1, axis_direction)
    two_ahead = jnp.roll(values, -2, axis_direction)
    two_behind = jnp.roll(values, 2, axis_direction)
    return (8.0 * (step_ahead - step_behind) - (two_ahead - two_behind)) / 12.0


def reference(packed_state_matrix, energies, dipole_x, dipole_y, interaction, driving_field):
    primitive_tile_total = NKX * NKY
    gradient_x = grid_derivative(packed_state_matrix, 1)
    gradient_y = grid_derivative(packed_state_matrix, 2)
    velocity_x = grid_derivative(energies, 1)
    group_velocity_y = grid_derivative(energies, 2)
    electron_population = jnp.sum(packed_state_matrix[2] + packed_state_matrix[3]) / primitive_tile_total
    current_x = jnp.sum(velocity_x * packed_state_matrix[0:4]) / primitive_tile_total
    current_y = jnp.sum(group_velocity_y * packed_state_matrix[0:4]) / primitive_tile_total
    shielding_multiplier = 1.0 / (1.0 + SHIELDING_LEVEL * electron_population)

    def convolve_one(component):
        spectrum = jnp.fft.fft2(component) * interaction
        return jnp.real(jnp.fft.ifft2(spectrum)).astype(jnp.float32)

    convolved = lax.map(convolve_one, packed_state_matrix)
    self_energy = -shielding_multiplier * convolved
    section_slope = slope_terms(packed_state_matrix, energies, self_energy, gradient_x, gradient_y, dipole_x, dipole_y, driving_field)
    field_next = driving_field - COUPLING * jnp.stack([current_x, current_y])
    return section_slope, field_next
```

```python
import math

import jax
import jax.numpy as jnp
from jax import lax
from jax.sharding import PartitionSpec as P

BAND_PAIRS = ((0, 1), (0, 2), (0, 3), (1, 2), (1, 3), (2, 3))
DEPHASING = 0.5
SHIELDING_LEVEL = 2.0
COUPLING = 40.0


def unpack(packed):
    real_entries = []
    imaginary_entries = []
    for band_one in range(4):
        real_entries.append([None, None, None, None])
        imaginary_entries.append([None, None, None, None])
    for band_one in range(4):
        real_entries[band_one][band_one] = packed[band_one]
    for number, band_pair in enumerate(BAND_PAIRS):
        upper_band, lower_band = band_pair
        real_entries[upper_band][lower_band] = packed[4 + number]
        real_entries[lower_band][upper_band] = packed[4 + number]
        imaginary_entries[upper_band][lower_band] = packed[10 + number]
        imaginary_entries[lower_band][upper_band] = -packed[10 + number]
    return (real_entries, imaginary_entries)


def product_sum(terms):
    summed = None
    for factor, left_value, right_value in terms:
        if left_value is None or right_value is None:
            continue
        product = factor * left_value * right_value
        summed = product if summed is None else summed + product
    return summed


def commutator(coupled, packed_state_matrix):
    coupled_real, coupled_imaginary = unpack(coupled)
    state_real, state_imaginary = unpack(packed_state_matrix)

    def element(row_band, column_band):
        real_terms = []
        imaginary_terms = []
        for middle in range(4):
            real_terms.append(
                (1.0, coupled_real[row_band][middle], state_real[middle][column_band])
            )
            real_terms.append(
                (-1.0, coupled_imaginary[row_band][middle], state_imaginary[middle][column_band])
            )
            real_terms.append(
                (-1.0, state_real[row_band][middle], coupled_real[middle][column_band])
            )
            real_terms.append(
                (1.0, state_imaginary[row_band][middle], coupled_imaginary[middle][column_band])
            )
            imaginary_terms.append(
                (1.0, coupled_real[row_band][middle], state_imaginary[middle][column_band])
            )
            imaginary_terms.append(
                (1.0, coupled_imaginary[row_band][middle], state_real[middle][column_band])
            )
            imaginary_terms.append(
                (-1.0, state_real[row_band][middle], coupled_imaginary[middle][column_band])
            )
            imaginary_terms.append(
                (-1.0, state_imaginary[row_band][middle], coupled_real[middle][column_band])
            )
        return (product_sum(real_terms), product_sum(imaginary_terms))

    diagonal = []
    upper_real = []
    upper_imaginary = []
    for band_one in range(4):
        diagonal.append(element(band_one, band_one)[1])
    for upper_band, lower_band in BAND_PAIRS:
        real_value, imaginary_value = element(upper_band, lower_band)
        upper_real.append(imaginary_value)
        upper_imaginary.append(-real_value)
    return jnp.stack(diagonal + upper_real + upper_imaginary)


def slope_terms(
    packed_state_matrix,
    energies,
    self_energy,
    gradient_x,
    gradient_y,
    dipole_x,
    dipole_y,
    driving_field,
):
    field_x = driving_field[0]
    field_y = driving_field[1]
    coupled = jnp.concatenate(
        [energies + self_energy[0:4], self_energy[4:16] + field_x * dipole_x + field_y * dipole_y]
    )
    rotation = commutator(coupled, packed_state_matrix)
    drift = rotation + field_x * gradient_x + field_y * gradient_y
    return jnp.concatenate([drift[0:4], drift[4:16] - DEPHASING * packed_state_matrix[4:16]])


def contract(einsum_form, left, right):
    return jnp.einsum(
        einsum_form, left, right, precision=lax.Precision.HIGHEST, preferred_element_type=jnp.float32
    )


def angles(row_count, column_count, period):
    row_index = lax.broadcasted_iota(jnp.int32, (row_count, column_count), 0)
    column_index = lax.broadcasted_iota(jnp.int32, (row_count, column_count), 1)
    return (row_index * column_index % period).astype(jnp.float32) * (2.0 * math.pi / period)


def hartley_tables(x_length, groups, group_length):
    x_angle = angles(x_length, x_length, x_length)
    group_angle = angles(groups, groups, groups)
    twist_angle = angles(groups, group_length, groups * group_length)
    inner_angle = angles(group_length, group_length, group_length)
    return dict(
        cas_x=jnp.cos(x_angle) + jnp.sin(x_angle),
        group_cos=jnp.cos(group_angle),
        group_sin=jnp.sin(group_angle),
        twist_cos=jnp.cos(twist_angle)[None, :, None, :],
        twist_sin=jnp.sin(twist_angle)[None, :, None, :],
        inner_plus=jnp.cos(inner_angle) + jnp.sin(inner_angle),
        inner_minus=jnp.cos(inner_angle) - jnp.sin(inner_angle),
    )


def hartley_y(data, tables):
    first_real = contract("ka,capb->ckpb", tables["group_cos"], data)
    first_imaginary = -contract("ka,capb->ckpb", tables["group_sin"], data)
    turned_real = first_real * tables["twist_cos"] + first_imaginary * tables["twist_sin"]
    turned_imaginary = first_imaginary * tables["twist_cos"] - first_real * tables["twist_sin"]
    return contract("ckpb,bq->ckpq", turned_real, tables["inner_plus"]) - contract(
        "ckpb,bq->ckpq", turned_imaginary, tables["inner_minus"]
    )


def hartley_y_transposed(data, tables):
    turned_real = contract("ckpq,bq->ckpb", data, tables["inner_plus"])
    turned_imaginary = -contract("ckpq,bq->ckpb", data, tables["inner_minus"])
    first_real = turned_real * tables["twist_cos"] - turned_imaginary * tables["twist_sin"]
    first_imaginary = turned_real * tables["twist_sin"] + turned_imaginary * tables["twist_cos"]
    return contract("ka,ckpb->capb", tables["group_cos"], first_real) - contract(
        "ka,ckpb->capb", tables["group_sin"], first_imaginary
    )


def convolve(source, interaction, primitive_tile_total):
    kx_devices = lax.axis_size("kx")
    ky_devices = lax.axis_size("ky")
    along_kx = lax.all_to_all(source, "kx", split_axis=0, concat_axis=1, tiled=True)
    components, x_length, column_count = along_kx.shape
    row_count = x_length // ky_devices
    tables = hartley_tables(x_length, ky_devices, column_count)
    rows_x = contract("px,cxy->cpy", tables["cas_x"], along_kx)
    split = rows_x.reshape(components, ky_devices, row_count, column_count)
    along_ky = lax.all_to_all(split, "ky", split_axis=1, concat_axis=1, tiled=True)
    spectrum = hartley_y(along_ky, tables)
    weight = interaction.reshape(row_count, column_count, ky_devices).transpose(2, 0, 1)
    weighted = spectrum * (weight * (1.0 / primitive_tile_total))[None]
    back_y = hartley_y_transposed(weighted, tables)
    returned = lax.all_to_all(back_y, "ky", split_axis=1, concat_axis=1, tiled=True)
    returned = returned.reshape(components, x_length, column_count)
    final = contract("px,cpy->cxy", tables["cas_x"], returned)
    final = final.reshape(components, kx_devices, x_length // kx_devices, column_count)
    back = lax.all_to_all(final, "kx", split_axis=1, concat_axis=0, tiled=True)
    return back.reshape(components * kx_devices, x_length // kx_devices, column_count)


def group_sum(values, axis):
    devices = lax.axis_size(axis)
    spread = jnp.broadcast_to(values[None], (devices,) + values.shape)
    gathered = lax.all_to_all(spread, axis, split_axis=0, concat_axis=0, tiled=True)
    return jnp.sum(gathered, axis=0)


def collect_moments(local_sums, primitive_tile_total):
    return group_sum(group_sum(local_sums, "ky"), "kx") / primitive_tile_total


def neighbours(array, axis, dim, width):
    devices, length = (lax.axis_size(axis), array.shape[dim])
    up = [(i, (i + 1) % devices) for i in range(devices)]
    down = [(j, i) for i, j in up]
    last = lax.slice_in_dim(array, length - width, length, axis=dim)
    initial = lax.slice_in_dim(array, 0, width, axis=dim)
    before = lax.ppermute(last, axis, up)
    after = lax.ppermute(initial, axis, down)
    return jnp.concatenate([before, array, after], axis=dim)


def body(packed_state_matrix, energies, dipole_x, dipole_y, interaction, driving_field):
    rows_local = packed_state_matrix.shape[1]
    columns_local = packed_state_matrix.shape[2]
    primitive_tile_total = rows_local * columns_local * lax.axis_size("kx") * lax.axis_size("ky")
    stacked = jnp.concatenate([packed_state_matrix, energies])
    column_core = neighbours(stacked, "kx", 1, 2)
    row_core = neighbours(stacked, "ky", 2, 2)
    gradient_x = (
        8.0 * (column_core[:, 3:-1] - column_core[:, 1:-3])
        - (column_core[:, 4:] - column_core[:, :-4])
    ) / 12.0
    gradient_y = (
        8.0 * (row_core[:, :, 3:-1] - row_core[:, :, 1:-3])
        - (row_core[:, :, 4:] - row_core[:, :, :-4])
    ) / 12.0
    populations = packed_state_matrix[0:4]
    local_sums = jnp.stack(
        [
            jnp.sum(packed_state_matrix[2] + packed_state_matrix[3]),
            jnp.sum(gradient_x[16:20] * populations),
            jnp.sum(gradient_y[16:20] * populations),
        ]
    )
    totals = collect_moments(local_sums, primitive_tile_total)
    shielding_multiplier = 1.0 / (1.0 + SHIELDING_LEVEL * totals[0])
    convolved = convolve(packed_state_matrix, interaction, primitive_tile_total)
    self_energy = -shielding_multiplier * convolved
    section_slope = slope_terms(
        packed_state_matrix,
        energies,
        self_energy,
        gradient_x[0:16],
        gradient_y[0:16],
        dipole_x,
        dipole_y,
        driving_field,
    )
    field_next = driving_field - COUPLING * totals[1:3]
    return (section_slope, field_next)


def solution(mesh):
    in_specs = (
        P(None, "kx", "ky"),
        P(None, "kx", "ky"),
        P(None, "kx", "ky"),
        P(None, "kx", "ky"),
        P("ky", None),
        P(),
    )
    out_specs = (P(None, "kx", "ky"), P())
    return jax.shard_map(body, mesh=mesh, in_specs=in_specs, out_specs=out_specs, check_vma=False)
```

```python
import math

import jax
import numpy as np
import jax.numpy as jnp
from jax import lax
from jax.sharding import PartitionSpec as P

BAND_PAIRS = ((0, 1), (0, 2), (0, 3), (1, 2), (1, 3), (2, 3))
DEPHASING = 0.5
SHIELDING_LEVEL = 2.0
COUPLING = 40.0


def unpack(packed):
    real_entries = []
    imaginary_entries = []
    for band_one in range(4):
        real_entries.append([None, None, None, None])
        imaginary_entries.append([None, None, None, None])
    for band_one in range(4):
        real_entries[band_one][band_one] = packed[band_one]
    for number, band_pair in enumerate(BAND_PAIRS):
        upper_band, lower_band = band_pair
        real_entries[upper_band][lower_band] = packed[4 + number]
        real_entries[lower_band][upper_band] = packed[4 + number]
        imaginary_entries[upper_band][lower_band] = packed[10 + number]
        imaginary_entries[lower_band][upper_band] = -packed[10 + number]
    return (real_entries, imaginary_entries)


def product_sum(terms):
    summed = None
    for factor, left_value, right_value in terms:
        if left_value is None or right_value is None:
            continue
        product = factor * left_value * right_value
        summed = product if summed is None else summed + product
    return summed


def commutator(coupled, packed_state_matrix):
    coupled_real, coupled_imaginary = unpack(coupled)
    state_real, state_imaginary = unpack(packed_state_matrix)

    def element(row_band, column_band):
        real_terms = []
        imaginary_terms = []
        for middle in range(4):
            real_terms.append(
                (1.0, coupled_real[row_band][middle], state_real[middle][column_band])
            )
            real_terms.append(
                (-1.0, coupled_imaginary[row_band][middle], state_imaginary[middle][column_band])
            )
            real_terms.append(
                (-1.0, state_real[row_band][middle], coupled_real[middle][column_band])
            )
            real_terms.append(
                (1.0, state_imaginary[row_band][middle], coupled_imaginary[middle][column_band])
            )
            imaginary_terms.append(
                (1.0, coupled_real[row_band][middle], state_imaginary[middle][column_band])
            )
            imaginary_terms.append(
                (1.0, coupled_imaginary[row_band][middle], state_real[middle][column_band])
            )
            imaginary_terms.append(
                (-1.0, state_real[row_band][middle], coupled_imaginary[middle][column_band])
            )
            imaginary_terms.append(
                (-1.0, state_imaginary[row_band][middle], coupled_real[middle][column_band])
            )
        return (product_sum(real_terms), product_sum(imaginary_terms))

    diagonal = []
    upper_real = []
    upper_imaginary = []
    for band_one in range(4):
        diagonal.append(element(band_one, band_one)[1])
    for upper_band, lower_band in BAND_PAIRS:
        real_value, imaginary_value = element(upper_band, lower_band)
        upper_real.append(imaginary_value)
        upper_imaginary.append(-real_value)
    return jnp.stack(diagonal + upper_real + upper_imaginary)


def slope_terms(
    packed_state_matrix,
    energies,
    self_energy,
    gradient_x,
    gradient_y,
    dipole_x,
    dipole_y,
    driving_field,
):
    field_x = driving_field[0]
    field_y = driving_field[1]
    coupled = jnp.concatenate(
        [energies + self_energy[0:4], self_energy[4:16] + field_x * dipole_x + field_y * dipole_y]
    )
    rotation = commutator(coupled, packed_state_matrix)
    drift = rotation + field_x * gradient_x + field_y * gradient_y
    return jnp.concatenate([drift[0:4], drift[4:16] - DEPHASING * packed_state_matrix[4:16]])


def contract(einsum_form, left, right):
    return jnp.einsum(
        einsum_form, left, right, precision=lax.Precision.HIGHEST, preferred_element_type=jnp.float32
    )


def angles(row_count, column_count, period):
    row_index = np.arange(row_count, dtype=np.int64)[:, None]
    column_index = np.arange(column_count, dtype=np.int64)[None, :]
    return (row_index * column_index % period).astype(np.float64) * (2.0 * math.pi / period)


def table(values):
    return jnp.asarray(values.astype(np.float32))


def hartley_tables(x_length, groups, group_length):
    x_angle = angles(x_length, x_length, x_length)
    group_angle = angles(groups, groups, groups)
    twist_angle = angles(groups, group_length, groups * group_length)
    inner_angle = angles(group_length, group_length, group_length)
    return dict(
        cas_x=table(np.cos(x_angle) + np.sin(x_angle)),
        group_cos=table(np.cos(group_angle)),
        group_sin=table(np.sin(group_angle)),
        twist_cos=table(np.cos(twist_angle)[None, :, None, :]),
        twist_sin=table(np.sin(twist_angle)[None, :, None, :]),
        inner_plus=table(np.cos(inner_angle) + np.sin(inner_angle)),
        inner_minus=table(np.cos(inner_angle) - np.sin(inner_angle)),
    )


def hartley_y(data, tables):
    first_real = contract("ka,capb->ckpb", tables["group_cos"], data)
    first_imaginary = -contract("ka,capb->ckpb", tables["group_sin"], data)
    turned_real = first_real * tables["twist_cos"] + first_imaginary * tables["twist_sin"]
    turned_imaginary = first_imaginary * tables["twist_cos"] - first_real * tables["twist_sin"]
    return contract("ckpb,bq->ckpq", turned_real, tables["inner_plus"]) - contract(
        "ckpb,bq->ckpq", turned_imaginary, tables["inner_minus"]
    )


def hartley_y_transposed(data, tables):
    turned_real = contract("ckpq,bq->ckpb", data, tables["inner_plus"])
    turned_imaginary = -contract("ckpq,bq->ckpb", data, tables["inner_minus"])
    first_real = turned_real * tables["twist_cos"] - turned_imaginary * tables["twist_sin"]
    first_imaginary = turned_real * tables["twist_sin"] + turned_imaginary * tables["twist_cos"]
    return contract("ka,ckpb->capb", tables["group_cos"], first_real) - contract(
        "ka,ckpb->capb", tables["group_sin"], first_imaginary
    )


def convolve(source, interaction, primitive_tile_total):
    kx_devices = lax.axis_size("kx")
    ky_devices = lax.axis_size("ky")
    along_kx = lax.all_to_all(source, "kx", split_axis=0, concat_axis=1, tiled=True)
    components, x_length, column_count = along_kx.shape
    row_count = x_length // ky_devices
    tables = hartley_tables(x_length, ky_devices, column_count)
    rows_x = contract("px,cxy->cpy", tables["cas_x"], along_kx)
    split = rows_x.reshape(components, ky_devices, row_count, column_count)
    along_ky = lax.all_to_all(split, "ky", split_axis=1, concat_axis=1, tiled=True)
    spectrum = hartley_y(along_ky, tables)
    weight = interaction.reshape(row_count, column_count, ky_devices).transpose(2, 0, 1)
    weighted = spectrum * (weight * (1.0 / primitive_tile_total))[None]
    back_y = hartley_y_transposed(weighted, tables)
    returned = lax.all_to_all(back_y, "ky", split_axis=1, concat_axis=1, tiled=True)
    returned = returned.reshape(components, x_length, column_count)
    final = contract("px,cpy->cxy", tables["cas_x"], returned)
    final = final.reshape(components, kx_devices, x_length // kx_devices, column_count)
    back = lax.all_to_all(final, "kx", split_axis=1, concat_axis=0, tiled=True)
    return back.reshape(components * kx_devices, x_length // kx_devices, column_count)


def group_sum(values, axis):
    devices = lax.axis_size(axis)
    spread = jnp.broadcast_to(values[None], (devices,) + values.shape)
    gathered = lax.all_to_all(spread, axis, split_axis=0, concat_axis=0, tiled=True)
    return jnp.sum(gathered, axis=0)


def collect_moments(local_sums, primitive_tile_total):
    return group_sum(group_sum(local_sums, "ky"), "kx") / primitive_tile_total


def neighbours(array, axis, dim, width):
    devices, length = (lax.axis_size(axis), array.shape[dim])
    up = [(i, (i + 1) % devices) for i in range(devices)]
    down = [(j, i) for i, j in up]
    last = lax.slice_in_dim(array, length - width, length, axis=dim)
    initial = lax.slice_in_dim(array, 0, width, axis=dim)
    dense = (-1, 128) if last.size % 128 == 0 else last.shape
    before = lax.ppermute(last.reshape(dense), axis, up).reshape(last.shape)
    after = lax.ppermute(initial.reshape(dense), axis, down).reshape(initial.shape)
    return jnp.concatenate([before, array, after], axis=dim)


def body(packed_state_matrix, energies, dipole_x, dipole_y, interaction, driving_field):
    rows_local = packed_state_matrix.shape[1]
    columns_local = packed_state_matrix.shape[2]
    primitive_tile_total = rows_local * columns_local * lax.axis_size("kx") * lax.axis_size("ky")
    stacked = jnp.concatenate([packed_state_matrix, energies])
    column_core = neighbours(stacked, "kx", 1, 2)
    row_core = neighbours(stacked, "ky", 2, 2)
    gradient_x = (
        8.0 * (column_core[:, 3:-1] - column_core[:, 1:-3])
        - (column_core[:, 4:] - column_core[:, :-4])
    ) / 12.0
    gradient_y = (
        8.0 * (row_core[:, :, 3:-1] - row_core[:, :, 1:-3])
        - (row_core[:, :, 4:] - row_core[:, :, :-4])
    ) / 12.0
    populations = packed_state_matrix[0:4]
    local_sums = jnp.stack(
        [
            jnp.sum(packed_state_matrix[2] + packed_state_matrix[3]),
            jnp.sum(gradient_x[16:20] * populations),
            jnp.sum(gradient_y[16:20] * populations),
        ]
    )
    totals = collect_moments(local_sums, primitive_tile_total)
    shielding_multiplier = 1.0 / (1.0 + SHIELDING_LEVEL * totals[0])
    convolved = convolve(packed_state_matrix, interaction, primitive_tile_total)
    self_energy = -shielding_multiplier * convolved
    section_slope = slope_terms(
        packed_state_matrix,
        energies,
        self_energy,
        gradient_x[0:16],
        gradient_y[0:16],
        dipole_x,
        dipole_y,
        driving_field,
    )
    field_next = driving_field - COUPLING * totals[1:3]
    return (section_slope, field_next)


def solution(mesh):
    in_specs = (
        P(None, "kx", "ky"),
        P(None, "kx", "ky"),
        P(None, "kx", "ky"),
        P(None, "kx", "ky"),
        P("ky", None),
        P(),
    )
    out_specs = (P(None, "kx", "ky"), P())
    return jax.shard_map(body, mesh=mesh, in_specs=in_specs, out_specs=out_specs, check_vma=False)
```

```python
import math

import jax
import numpy as np
import jax.numpy as jnp
from jax import lax
from jax.sharding import PartitionSpec as P

BAND_PAIRS = ((0, 1), (0, 2), (0, 3), (1, 2), (1, 3), (2, 3))
DEPHASING = 0.5
SHIELDING_LEVEL = 2.0
COUPLING = 40.0


def unpack(packed):
    real_entries = []
    imaginary_entries = []
    for band_one in range(4):
        real_entries.append([None, None, None, None])
        imaginary_entries.append([None, None, None, None])
    for band_one in range(4):
        real_entries[band_one][band_one] = packed[band_one]
    for number, band_pair in enumerate(BAND_PAIRS):
        upper_band, lower_band = band_pair
        real_entries[upper_band][lower_band] = packed[4 + number]
        real_entries[lower_band][upper_band] = packed[4 + number]
        imaginary_entries[upper_band][lower_band] = packed[10 + number]
        imaginary_entries[lower_band][upper_band] = -packed[10 + number]
    return (real_entries, imaginary_entries)


def product_sum(terms):
    summed = None
    for factor, left_value, right_value in terms:
        if left_value is None or right_value is None:
            continue
        product = factor * left_value * right_value
        summed = product if summed is None else summed + product
    return summed


def commutator(coupled, packed_state_matrix):
    coupled_real, coupled_imaginary = unpack(coupled)
    state_real, state_imaginary = unpack(packed_state_matrix)

    def element(row_band, column_band):
        real_terms = []
        imaginary_terms = []
        for middle in range(4):
            real_terms.append(
                (1.0, coupled_real[row_band][middle], state_real[middle][column_band])
            )
            real_terms.append(
                (-1.0, coupled_imaginary[row_band][middle], state_imaginary[middle][column_band])
            )
            real_terms.append(
                (-1.0, state_real[row_band][middle], coupled_real[middle][column_band])
            )
            real_terms.append(
                (1.0, state_imaginary[row_band][middle], coupled_imaginary[middle][column_band])
            )
            imaginary_terms.append(
                (1.0, coupled_real[row_band][middle], state_imaginary[middle][column_band])
            )
            imaginary_terms.append(
                (1.0, coupled_imaginary[row_band][middle], state_real[middle][column_band])
            )
            imaginary_terms.append(
                (-1.0, state_real[row_band][middle], coupled_imaginary[middle][column_band])
            )
            imaginary_terms.append(
                (-1.0, state_imaginary[row_band][middle], coupled_real[middle][column_band])
            )
        return (product_sum(real_terms), product_sum(imaginary_terms))

    diagonal = []
    upper_real = []
    upper_imaginary = []
    for band_one in range(4):
        diagonal.append(element(band_one, band_one)[1])
    for upper_band, lower_band in BAND_PAIRS:
        real_value, imaginary_value = element(upper_band, lower_band)
        upper_real.append(imaginary_value)
        upper_imaginary.append(-real_value)
    return jnp.stack(diagonal + upper_real + upper_imaginary)


def slope_terms(
    packed_state_matrix,
    energies,
    self_energy,
    gradient_x,
    gradient_y,
    dipole_x,
    dipole_y,
    driving_field,
):
    field_x = driving_field[0]
    field_y = driving_field[1]
    coupled = jnp.concatenate(
        [energies + self_energy[0:4], self_energy[4:16] + field_x * dipole_x + field_y * dipole_y]
    )
    rotation = commutator(coupled, packed_state_matrix)
    drift = rotation + field_x * gradient_x + field_y * gradient_y
    return jnp.concatenate([drift[0:4], drift[4:16] - DEPHASING * packed_state_matrix[4:16]])


def contract(einsum_form, left, right):
    return jnp.einsum(
        einsum_form, left, right, precision=lax.Precision.HIGHEST, preferred_element_type=jnp.float32
    )


def angles(row_count, column_count, period):
    row_index = np.arange(row_count, dtype=np.int64)[:, None]
    column_index = np.arange(column_count, dtype=np.int64)[None, :]
    return (row_index * column_index % period).astype(np.float64) * (2.0 * math.pi / period)


def table(values):
    return jnp.asarray(values.astype(np.float32))


def hartley_tables(x_length, groups, group_length):
    x_angle = angles(x_length, x_length, x_length)
    group_angle = angles(groups, groups, groups)
    twist_angle = angles(groups, group_length, groups * group_length)
    inner_angle = angles(group_length, group_length, group_length)
    return dict(
        cas_x=table(np.cos(x_angle) + np.sin(x_angle)),
        group_cos=table(np.cos(group_angle)),
        group_sin=table(np.sin(group_angle)),
        twist_cos=table(np.cos(twist_angle)[None, :, None, :]),
        twist_sin=table(np.sin(twist_angle)[None, :, None, :]),
        inner_plus=table(np.cos(inner_angle) + np.sin(inner_angle)),
        inner_minus=table(np.cos(inner_angle) - np.sin(inner_angle)),
    )


def hartley_y(data, tables):
    first_real = contract("ka,capb->ckpb", tables["group_cos"], data)
    first_imaginary = -contract("ka,capb->ckpb", tables["group_sin"], data)
    turned_real = first_real * tables["twist_cos"] + first_imaginary * tables["twist_sin"]
    turned_imaginary = first_imaginary * tables["twist_cos"] - first_real * tables["twist_sin"]
    return contract("ckpb,bq->ckpq", turned_real, tables["inner_plus"]) - contract(
        "ckpb,bq->ckpq", turned_imaginary, tables["inner_minus"]
    )


def hartley_y_transposed(data, tables):
    turned_real = contract("ckpq,bq->ckpb", data, tables["inner_plus"])
    turned_imaginary = -contract("ckpq,bq->ckpb", data, tables["inner_minus"])
    first_real = turned_real * tables["twist_cos"] - turned_imaginary * tables["twist_sin"]
    first_imaginary = turned_real * tables["twist_sin"] + turned_imaginary * tables["twist_cos"]
    return contract("ka,ckpb->capb", tables["group_cos"], first_real) - contract(
        "ka,ckpb->capb", tables["group_sin"], first_imaginary
    )


def with_sums(data, sums, dim):
    shape = list(data.shape)
    shape[dim] = 8
    tile = jnp.zeros((8, data.shape[-1]), jnp.float32).at[0, 0 : sums.shape[0]].set(sums)
    return jnp.concatenate([data, jnp.broadcast_to(tile.reshape([1] * (data.ndim - 2) + [8, -1]), shape)], axis=dim)


def convolve_and_sum(source, interaction, local_sums, primitive_tile_total):
    kx_devices = lax.axis_size("kx")
    ky_devices = lax.axis_size("ky")
    sum_count = local_sums.shape[0]
    along_kx = lax.all_to_all(source, "kx", split_axis=0, concat_axis=1, tiled=True)
    components, x_length, column_count = along_kx.shape
    row_count = x_length // ky_devices
    tables = hartley_tables(x_length, ky_devices, column_count)
    rows_x = contract("px,cxy->cpy", tables["cas_x"], along_kx)
    split = with_sums(rows_x.reshape(components, ky_devices, row_count, column_count), local_sums, 2)
    along_ky = lax.all_to_all(split, "ky", split_axis=1, concat_axis=1, tiled=True)
    ky_sums = jnp.sum(along_ky[0, :, row_count, 0:sum_count], axis=0)
    spectrum = hartley_y(along_ky[:, :, 0:row_count], tables)
    weight = interaction.reshape(row_count, column_count, ky_devices).transpose(2, 0, 1)
    weighted = spectrum * (weight * (1.0 / primitive_tile_total))[None]
    back_y = hartley_y_transposed(weighted, tables)
    returned = lax.all_to_all(back_y, "ky", split_axis=1, concat_axis=1, tiled=True)
    returned = returned.reshape(components, x_length, column_count)
    final = contract("px,cpy->cxy", tables["cas_x"], returned)
    rows_local = x_length // kx_devices
    final = with_sums(final.reshape(components, kx_devices, rows_local, column_count), ky_sums, 2)
    back = lax.all_to_all(final, "kx", split_axis=1, concat_axis=0, tiled=True)
    totals = jnp.sum(back[::components, 0, rows_local, 0:sum_count], axis=0) / primitive_tile_total
    convolved = back[:, 0, 0:rows_local].reshape(components * kx_devices, rows_local, column_count)
    return convolved, totals


def neighbours(array, axis, dim, width):
    devices, length = (lax.axis_size(axis), array.shape[dim])
    up = [(i, (i + 1) % devices) for i in range(devices)]
    down = [(j, i) for i, j in up]
    last = lax.slice_in_dim(array, length - width, length, axis=dim)
    initial = lax.slice_in_dim(array, 0, width, axis=dim)
    dense = (-1, 128) if last.size % 128 == 0 else last.shape
    before = lax.ppermute(last.reshape(dense), axis, up).reshape(last.shape)
    after = lax.ppermute(initial.reshape(dense), axis, down).reshape(initial.shape)
    return jnp.concatenate([before, array, after], axis=dim)


def body(packed_state_matrix, energies, dipole_x, dipole_y, interaction, driving_field):
    rows_local = packed_state_matrix.shape[1]
    columns_local = packed_state_matrix.shape[2]
    primitive_tile_total = rows_local * columns_local * lax.axis_size("kx") * lax.axis_size("ky")
    stacked = jnp.concatenate([packed_state_matrix, energies])
    column_core = neighbours(stacked, "kx", 1, 2)
    row_core = neighbours(stacked, "ky", 2, 2)
    gradient_x = (
        8.0 * (column_core[:, 3:-1] - column_core[:, 1:-3])
        - (column_core[:, 4:] - column_core[:, :-4])
    ) / 12.0
    gradient_y = (
        8.0 * (row_core[:, :, 3:-1] - row_core[:, :, 1:-3])
        - (row_core[:, :, 4:] - row_core[:, :, :-4])
    ) / 12.0
    populations = packed_state_matrix[0:4]
    local_sums = jnp.stack(
        [
            jnp.sum(packed_state_matrix[2] + packed_state_matrix[3]),
            jnp.sum(gradient_x[16:20] * populations),
            jnp.sum(gradient_y[16:20] * populations),
        ]
    )
    convolved, totals = convolve_and_sum(
        packed_state_matrix, interaction, local_sums, primitive_tile_total
    )
    shielding_multiplier = 1.0 / (1.0 + SHIELDING_LEVEL * totals[0])
    self_energy = -shielding_multiplier * convolved
    section_slope = slope_terms(
        packed_state_matrix,
        energies,
        self_energy,
        gradient_x[0:16],
        gradient_y[0:16],
        dipole_x,
        dipole_y,
        driving_field,
    )
    field_next = driving_field - COUPLING * totals[1:3]
    return (section_slope, field_next)


def solution(mesh):
    in_specs = (
        P(None, "kx", "ky"),
        P(None, "kx", "ky"),
        P(None, "kx", "ky"),
        P(None, "kx", "ky"),
        P("ky", None),
        P(),
    )
    out_specs = (P(None, "kx", "ky"), P())
    return jax.shard_map(body, mesh=mesh, in_specs=in_specs, out_specs=out_specs, check_vma=False)
```

```python
import math

import jax
import numpy as np
import jax.numpy as jnp
from jax import lax
from jax.sharding import PartitionSpec as P

BAND_PAIRS = ((0, 1), (0, 2), (0, 3), (1, 2), (1, 3), (2, 3))
DEPHASING = 0.5
SHIELDING_LEVEL = 2.0
COUPLING = 40.0


def unpack(packed):
    real_entries = []
    imaginary_entries = []
    for band_one in range(4):
        real_entries.append([None, None, None, None])
        imaginary_entries.append([None, None, None, None])
    for band_one in range(4):
        real_entries[band_one][band_one] = packed[band_one]
    for number, band_pair in enumerate(BAND_PAIRS):
        upper_band, lower_band = band_pair
        real_entries[upper_band][lower_band] = packed[4 + number]
        real_entries[lower_band][upper_band] = packed[4 + number]
        imaginary_entries[upper_band][lower_band] = packed[10 + number]
        imaginary_entries[lower_band][upper_band] = -packed[10 + number]
    return (real_entries, imaginary_entries)


def product_sum(terms):
    summed = None
    for factor, left_value, right_value in terms:
        if left_value is None or right_value is None:
            continue
        product = factor * left_value * right_value
        summed = product if summed is None else summed + product
    return summed


def commutator(coupled, packed_state_matrix):
    coupled_real, coupled_imaginary = unpack(coupled)
    state_real, state_imaginary = unpack(packed_state_matrix)

    def element(row_band, column_band):
        real_terms = []
        imaginary_terms = []
        for middle in range(4):
            real_terms.append(
                (1.0, coupled_real[row_band][middle], state_real[middle][column_band])
            )
            real_terms.append(
                (-1.0, coupled_imaginary[row_band][middle], state_imaginary[middle][column_band])
            )
            real_terms.append(
                (-1.0, state_real[row_band][middle], coupled_real[middle][column_band])
            )
            real_terms.append(
                (1.0, state_imaginary[row_band][middle], coupled_imaginary[middle][column_band])
            )
            imaginary_terms.append(
                (1.0, coupled_real[row_band][middle], state_imaginary[middle][column_band])
            )
            imaginary_terms.append(
                (1.0, coupled_imaginary[row_band][middle], state_real[middle][column_band])
            )
            imaginary_terms.append(
                (-1.0, state_real[row_band][middle], coupled_imaginary[middle][column_band])
            )
            imaginary_terms.append(
                (-1.0, state_imaginary[row_band][middle], coupled_real[middle][column_band])
            )
        return (product_sum(real_terms), product_sum(imaginary_terms))

    diagonal = []
    upper_real = []
    upper_imaginary = []
    for band_one in range(4):
        diagonal.append(element(band_one, band_one)[1])
    for upper_band, lower_band in BAND_PAIRS:
        real_value, imaginary_value = element(upper_band, lower_band)
        upper_real.append(imaginary_value)
        upper_imaginary.append(-real_value)
    return jnp.stack(diagonal + upper_real + upper_imaginary)


def slope_terms(
    packed_state_matrix,
    energies,
    self_energy,
    gradient_x,
    gradient_y,
    dipole_x,
    dipole_y,
    driving_field,
):
    field_x = driving_field[0]
    field_y = driving_field[1]
    coupled = jnp.concatenate(
        [energies + self_energy[0:4], self_energy[4:16] + field_x * dipole_x + field_y * dipole_y]
    )
    rotation = commutator(coupled, packed_state_matrix)
    drift = rotation + field_x * gradient_x + field_y * gradient_y
    return jnp.concatenate([drift[0:4], drift[4:16] - DEPHASING * packed_state_matrix[4:16]])


def contract(einsum_form, left, right):
    return jnp.einsum(
        einsum_form, left, right, precision=lax.Precision.HIGHEST, preferred_element_type=jnp.float32
    )


def angles(row_count, column_count, period):
    row_index = np.arange(row_count, dtype=np.int64)[:, None]
    column_index = np.arange(column_count, dtype=np.int64)[None, :]
    return (row_index * column_index % period).astype(np.float64) * (2.0 * math.pi / period)


def table(values):
    return jnp.asarray(values.astype(np.float32))


def hartley_tables(x_length, groups, group_length):
    x_angle = angles(x_length, x_length, x_length)
    group_angle = angles(groups, groups, groups)
    twist_angle = angles(groups, group_length, groups * group_length)
    inner_angle = angles(group_length, group_length, group_length)
    return dict(
        cas_x=table(np.cos(x_angle) + np.sin(x_angle)),
        group_cos=table(np.cos(group_angle)),
        group_sin=table(np.sin(group_angle)),
        twist_cos=table(np.cos(twist_angle)[None, :, None, :]),
        twist_sin=table(np.sin(twist_angle)[None, :, None, :]),
        inner_plus=table(np.cos(inner_angle) + np.sin(inner_angle)),
        inner_minus=table(np.cos(inner_angle) - np.sin(inner_angle)),
    )


def hartley_y(data, tables):
    first_real = contract("ka,capb->ckpb", tables["group_cos"], data)
    first_imaginary = -contract("ka,capb->ckpb", tables["group_sin"], data)
    turned_real = first_real * tables["twist_cos"] + first_imaginary * tables["twist_sin"]
    turned_imaginary = first_imaginary * tables["twist_cos"] - first_real * tables["twist_sin"]
    return contract("ckpb,bq->ckpq", turned_real, tables["inner_plus"]) - contract(
        "ckpb,bq->ckpq", turned_imaginary, tables["inner_minus"]
    )


def hartley_y_transposed(data, tables):
    turned_real = contract("ckpq,bq->ckpb", data, tables["inner_plus"])
    turned_imaginary = -contract("ckpq,bq->ckpb", data, tables["inner_minus"])
    first_real = turned_real * tables["twist_cos"] - turned_imaginary * tables["twist_sin"]
    first_imaginary = turned_real * tables["twist_sin"] + turned_imaginary * tables["twist_cos"]
    return contract("ka,ckpb->capb", tables["group_cos"], first_real) - contract(
        "ka,ckpb->capb", tables["group_sin"], first_imaginary
    )


def with_sums(data, sums, dim):
    shape = list(data.shape)
    shape[dim] = 8
    tile = jnp.zeros((8, data.shape[-1]), jnp.float32).at[0, 0 : sums.shape[0]].set(sums)
    return jnp.concatenate([data, jnp.broadcast_to(tile.reshape([1] * (data.ndim - 2) + [8, -1]), shape)], axis=dim)


def convolve_and_sum(source, interaction, local_sums, after_transform, primitive_tile_total):
    kx_devices = lax.axis_size("kx")
    ky_devices = lax.axis_size("ky")
    sum_count = 3
    along_kx = lax.all_to_all(source, "kx", split_axis=0, concat_axis=1, tiled=True)
    components, x_length, column_count = along_kx.shape
    row_count = x_length // ky_devices
    tables = hartley_tables(x_length, ky_devices, column_count)
    rows_x = contract("px,cxy->cpy", tables["cas_x"], along_kx)
    rows_x = after_transform(rows_x)
    split = rows_x.reshape(components, ky_devices, row_count, column_count)
    along_ky = lax.all_to_all(split, "ky", split_axis=1, concat_axis=1, tiled=True)
    spectrum = hartley_y(along_ky, tables)
    weight = interaction.reshape(row_count, column_count, ky_devices).transpose(2, 0, 1)
    weighted = spectrum * (weight * (1.0 / primitive_tile_total))[None]
    back_y = with_sums(hartley_y_transposed(weighted, tables), local_sums(), 2)
    returned = lax.all_to_all(back_y, "ky", split_axis=1, concat_axis=1, tiled=True)
    ky_sums = jnp.sum(returned[0, :, row_count, 0:sum_count], axis=0)
    returned = returned[:, :, 0:row_count].reshape(components, x_length, column_count)
    final = contract("px,cpy->cxy", tables["cas_x"], returned)
    rows_local = x_length // kx_devices
    final = with_sums(final.reshape(components, kx_devices, rows_local, column_count), ky_sums, 2)
    back = lax.all_to_all(final, "kx", split_axis=1, concat_axis=0, tiled=True)
    totals = jnp.sum(back[::components, 0, rows_local, 0:sum_count], axis=0) / primitive_tile_total
    convolved = back[:, 0, 0:rows_local].reshape(components * kx_devices, rows_local, column_count)
    return convolved, totals


def neighbours(array, axis, dim, width):
    devices, length = (lax.axis_size(axis), array.shape[dim])
    up = [(i, (i + 1) % devices) for i in range(devices)]
    down = [(j, i) for i, j in up]
    last = lax.slice_in_dim(array, length - width, length, axis=dim)
    initial = lax.slice_in_dim(array, 0, width, axis=dim)
    dense = (-1, 128) if last.size % 128 == 0 else last.shape
    before = lax.ppermute(last.reshape(dense), axis, up).reshape(last.shape)
    after = lax.ppermute(initial.reshape(dense), axis, down).reshape(initial.shape)
    return jnp.concatenate([before, array, after], axis=dim)


def body(packed_state_matrix, energies, dipole_x, dipole_y, interaction, driving_field):
    rows_local = packed_state_matrix.shape[1]
    columns_local = packed_state_matrix.shape[2]
    primitive_tile_total = rows_local * columns_local * lax.axis_size("kx") * lax.axis_size("ky")
    populations = packed_state_matrix[0:4]
    halo_source = []
    gradients = []

    def after_transform(rows_x):
        rows_x, late = lax.optimization_barrier((rows_x, jnp.concatenate([packed_state_matrix, energies])))
        halo_source.append(late)
        return rows_x

    def local_sums():
        stacked = halo_source[0]
        column_core = neighbours(stacked, "kx", 1, 2)
        row_core = neighbours(stacked, "ky", 2, 2)
        gradient_x = (
            8.0 * (column_core[:, 3:-1] - column_core[:, 1:-3])
            - (column_core[:, 4:] - column_core[:, :-4])
        ) / 12.0
        gradient_y = (
            8.0 * (row_core[:, :, 3:-1] - row_core[:, :, 1:-3])
            - (row_core[:, :, 4:] - row_core[:, :, :-4])
        ) / 12.0
        gradients.extend([gradient_x, gradient_y])
        return jnp.stack(
            [
                jnp.sum(packed_state_matrix[2] + packed_state_matrix[3]),
                jnp.sum(gradient_x[16:20] * populations),
                jnp.sum(gradient_y[16:20] * populations),
            ]
        )

    convolved, totals = convolve_and_sum(
        packed_state_matrix, interaction, local_sums, after_transform, primitive_tile_total
    )
    gradient_x, gradient_y = gradients
    shielding_multiplier = 1.0 / (1.0 + SHIELDING_LEVEL * totals[0])
    self_energy = -shielding_multiplier * convolved
    section_slope = slope_terms(
        packed_state_matrix,
        energies,
        self_energy,
        gradient_x[0:16],
        gradient_y[0:16],
        dipole_x,
        dipole_y,
        driving_field,
    )
    field_next = driving_field - COUPLING * totals[1:3]
    return (section_slope, field_next)


def solution(mesh):
    in_specs = (
        P(None, "kx", "ky"),
        P(None, "kx", "ky"),
        P(None, "kx", "ky"),
        P(None, "kx", "ky"),
        P("ky", None),
        P(),
    )
    out_specs = (P(None, "kx", "ky"), P())
    return jax.shard_map(body, mesh=mesh, in_specs=in_specs, out_specs=out_specs, check_vma=False)
```

```python
import math

import jax
import numpy as np
import jax.numpy as jnp
from jax import lax
from jax.sharding import PartitionSpec as P

BAND_PAIRS = ((0, 1), (0, 2), (0, 3), (1, 2), (1, 3), (2, 3))
DEPHASING = 0.5
SHIELDING_LEVEL = 2.0
COUPLING = 40.0


def unpack(packed):
    real_entries = []
    imaginary_entries = []
    for band_one in range(4):
        real_entries.append([None, None, None, None])
        imaginary_entries.append([None, None, None, None])
    for band_one in range(4):
        real_entries[band_one][band_one] = packed[band_one]
    for number, band_pair in enumerate(BAND_PAIRS):
        upper_band, lower_band = band_pair
        real_entries[upper_band][lower_band] = packed[4 + number]
        real_entries[lower_band][upper_band] = packed[4 + number]
        imaginary_entries[upper_band][lower_band] = packed[10 + number]
        imaginary_entries[lower_band][upper_band] = -packed[10 + number]
    return (real_entries, imaginary_entries)


def product_sum(terms):
    summed = None
    for factor, left_value, right_value in terms:
        if left_value is None or right_value is None:
            continue
        product = factor * left_value * right_value
        summed = product if summed is None else summed + product
    return summed


def commutator(coupled, packed_state_matrix):
    coupled_real, coupled_imaginary = unpack(coupled)
    state_real, state_imaginary = unpack(packed_state_matrix)

    def element(row_band, column_band):
        real_terms = []
        imaginary_terms = []
        for middle in range(4):
            real_terms.append(
                (1.0, coupled_real[row_band][middle], state_real[middle][column_band])
            )
            real_terms.append(
                (-1.0, coupled_imaginary[row_band][middle], state_imaginary[middle][column_band])
            )
            real_terms.append(
                (-1.0, state_real[row_band][middle], coupled_real[middle][column_band])
            )
            real_terms.append(
                (1.0, state_imaginary[row_band][middle], coupled_imaginary[middle][column_band])
            )
            imaginary_terms.append(
                (1.0, coupled_real[row_band][middle], state_imaginary[middle][column_band])
            )
            imaginary_terms.append(
                (1.0, coupled_imaginary[row_band][middle], state_real[middle][column_band])
            )
            imaginary_terms.append(
                (-1.0, state_real[row_band][middle], coupled_imaginary[middle][column_band])
            )
            imaginary_terms.append(
                (-1.0, state_imaginary[row_band][middle], coupled_real[middle][column_band])
            )
        return (product_sum(real_terms), product_sum(imaginary_terms))

    diagonal = []
    upper_real = []
    upper_imaginary = []
    for band_one in range(4):
        diagonal.append(element(band_one, band_one)[1])
    for upper_band, lower_band in BAND_PAIRS:
        real_value, imaginary_value = element(upper_band, lower_band)
        upper_real.append(imaginary_value)
        upper_imaginary.append(-real_value)
    return jnp.stack(diagonal + upper_real + upper_imaginary)


def slope_terms(
    packed_state_matrix,
    energies,
    self_energy,
    gradient_x,
    gradient_y,
    dipole_x,
    dipole_y,
    driving_field,
):
    field_x = driving_field[0]
    field_y = driving_field[1]
    coupled = jnp.concatenate(
        [energies + self_energy[0:4], self_energy[4:16] + field_x * dipole_x + field_y * dipole_y]
    )
    rotation = commutator(coupled, packed_state_matrix)
    drift = rotation + field_x * gradient_x + field_y * gradient_y
    return jnp.concatenate([drift[0:4], drift[4:16] - DEPHASING * packed_state_matrix[4:16]])


def contract(einsum_form, left, right):
    return jnp.einsum(
        einsum_form, left, right, precision=lax.Precision.HIGHEST, preferred_element_type=jnp.float32
    )


def angles(row_count, column_count, period):
    row_index = np.arange(row_count, dtype=np.int64)[:, None]
    column_index = np.arange(column_count, dtype=np.int64)[None, :]
    return (row_index * column_index % period).astype(np.float64) * (2.0 * math.pi / period)


def table(values):
    return jnp.asarray(values.astype(np.float32))


def hartley_tables(x_length, groups, group_length):
    x_angle = angles(x_length, x_length, x_length)
    group_angle = angles(groups, groups, groups)
    twist_angle = angles(groups, group_length, groups * group_length)
    inner_angle = angles(group_length, group_length, group_length)
    return dict(
        cas_x=table(np.cos(x_angle) + np.sin(x_angle)),
        group_cos=table(np.cos(group_angle)),
        group_sin=table(np.sin(group_angle)),
        twist_cos=table(np.cos(twist_angle)[None, :, None, :]),
        twist_sin=table(np.sin(twist_angle)[None, :, None, :]),
        inner_plus=table(np.cos(inner_angle) + np.sin(inner_angle)),
        inner_minus=table(np.cos(inner_angle) - np.sin(inner_angle)),
    )


def hartley_y(data, tables):
    first_real = contract("ka,capb->ckpb", tables["group_cos"], data)
    first_imaginary = -contract("ka,capb->ckpb", tables["group_sin"], data)
    turned_real = first_real * tables["twist_cos"] + first_imaginary * tables["twist_sin"]
    turned_imaginary = first_imaginary * tables["twist_cos"] - first_real * tables["twist_sin"]
    return contract("ckpb,bq->ckpq", turned_real, tables["inner_plus"]) - contract(
        "ckpb,bq->ckpq", turned_imaginary, tables["inner_minus"]
    )


def hartley_y_transposed(data, tables):
    turned_real = contract("ckpq,bq->ckpb", data, tables["inner_plus"])
    turned_imaginary = -contract("ckpq,bq->ckpb", data, tables["inner_minus"])
    first_real = turned_real * tables["twist_cos"] - turned_imaginary * tables["twist_sin"]
    first_imaginary = turned_real * tables["twist_sin"] + turned_imaginary * tables["twist_cos"]
    return contract("ka,ckpb->capb", tables["group_cos"], first_real) - contract(
        "ka,ckpb->capb", tables["group_sin"], first_imaginary
    )


def with_sums(data, sums, dim):
    shape = list(data.shape)
    shape[dim] = 8
    tile = jnp.zeros((8, data.shape[-1]), jnp.float32).at[0, 0 : sums.shape[0]].set(sums)
    return jnp.concatenate([data, jnp.broadcast_to(tile.reshape([1] * (data.ndim - 2) + [8, -1]), shape)], axis=dim)


def convolve_and_sum(source, interaction, local_sums, after_transform, primitive_tile_total):
    kx_devices = lax.axis_size("kx")
    ky_devices = lax.axis_size("ky")
    sum_count = 3
    along_kx = lax.all_to_all(source, "kx", split_axis=0, concat_axis=1, tiled=True)
    components, x_length, column_count = along_kx.shape
    row_count = x_length // ky_devices
    tables = hartley_tables(x_length, ky_devices, column_count)
    rows_x = contract("px,cxy->cpy", tables["cas_x"], along_kx)
    rows_x = after_transform(rows_x)
    split = rows_x.reshape(components, ky_devices, row_count, column_count)
    along_ky = lax.all_to_all(split, "ky", split_axis=1, concat_axis=1, tiled=True)
    spectrum = hartley_y(along_ky, tables)
    weight = interaction.reshape(row_count, column_count, ky_devices).transpose(2, 0, 1)
    weighted = spectrum * (weight * (1.0 / primitive_tile_total))[None]
    ky_sums = lax.psum(local_sums(), "ky")
    back_y = hartley_y_transposed(weighted, tables)
    returned = lax.all_to_all(back_y, "ky", split_axis=1, concat_axis=1, tiled=True)
    returned = returned.reshape(components, x_length, column_count)
    final = contract("px,cpy->cxy", tables["cas_x"], returned)
    rows_local = x_length // kx_devices
    final = with_sums(final.reshape(components, kx_devices, rows_local, column_count), ky_sums, 2)
    back = lax.all_to_all(final, "kx", split_axis=1, concat_axis=0, tiled=True)
    totals = jnp.sum(back[::components, 0, rows_local, 0:sum_count], axis=0) / primitive_tile_total
    convolved = back[:, 0, 0:rows_local].reshape(components * kx_devices, rows_local, column_count)
    return convolved, totals


def neighbours(array, axis, dim, width):
    devices, length = (lax.axis_size(axis), array.shape[dim])
    up = [(i, (i + 1) % devices) for i in range(devices)]
    down = [(j, i) for i, j in up]
    last = lax.slice_in_dim(array, length - width, length, axis=dim)
    initial = lax.slice_in_dim(array, 0, width, axis=dim)
    dense = (-1, 128) if last.size % 128 == 0 else last.shape
    before = lax.ppermute(last.reshape(dense), axis, up).reshape(last.shape)
    after = lax.ppermute(initial.reshape(dense), axis, down).reshape(initial.shape)
    return jnp.concatenate([before, array, after], axis=dim)


def body(packed_state_matrix, energies, dipole_x, dipole_y, interaction, driving_field):
    rows_local = packed_state_matrix.shape[1]
    columns_local = packed_state_matrix.shape[2]
    primitive_tile_total = rows_local * columns_local * lax.axis_size("kx") * lax.axis_size("ky")
    populations = packed_state_matrix[0:4]
    halo_source = []
    gradients = []

    def after_transform(rows_x):
        rows_x, late = lax.optimization_barrier((rows_x, jnp.concatenate([packed_state_matrix, energies])))
        halo_source.append(late)
        return rows_x

    def local_sums():
        stacked = halo_source[0]
        column_core = neighbours(stacked, "kx", 1, 2)
        row_core = neighbours(stacked, "ky", 2, 2)
        gradient_x = (
            8.0 * (column_core[:, 3:-1] - column_core[:, 1:-3])
            - (column_core[:, 4:] - column_core[:, :-4])
        ) / 12.0
        gradient_y = (
            8.0 * (row_core[:, :, 3:-1] - row_core[:, :, 1:-3])
            - (row_core[:, :, 4:] - row_core[:, :, :-4])
        ) / 12.0
        gradients.extend([gradient_x, gradient_y])
        return jnp.stack(
            [
                jnp.sum(packed_state_matrix[2] + packed_state_matrix[3]),
                jnp.sum(gradient_x[16:20] * populations),
                jnp.sum(gradient_y[16:20] * populations),
            ]
        )

    convolved, totals = convolve_and_sum(
        packed_state_matrix, interaction, local_sums, after_transform, primitive_tile_total
    )
    gradient_x, gradient_y = gradients
    shielding_multiplier = 1.0 / (1.0 + SHIELDING_LEVEL * totals[0])
    self_energy = -shielding_multiplier * convolved
    section_slope = slope_terms(
        packed_state_matrix,
        energies,
        self_energy,
        gradient_x[0:16],
        gradient_y[0:16],
        dipole_x,
        dipole_y,
        driving_field,
    )
    field_next = driving_field - COUPLING * totals[1:3]
    return (section_slope, field_next)


def solution(mesh):
    in_specs = (
        P(None, "kx", "ky"),
        P(None, "kx", "ky"),
        P(None, "kx", "ky"),
        P(None, "kx", "ky"),
        P("ky", None),
        P(),
    )
    out_specs = (P(None, "kx", "ky"), P())
    return jax.shard_map(body, mesh=mesh, in_specs=in_specs, out_specs=out_specs, check_vma=False)
```

```python
import math

import jax
import numpy as np
import jax.numpy as jnp
from jax import lax
from jax.sharding import PartitionSpec as P

BAND_PAIRS = ((0, 1), (0, 2), (0, 3), (1, 2), (1, 3), (2, 3))
DEPHASING = 0.5
SHIELDING_LEVEL = 2.0
COUPLING = 40.0


def unpack(packed):
    real_entries = []
    imaginary_entries = []
    for band_one in range(4):
        real_entries.append([None, None, None, None])
        imaginary_entries.append([None, None, None, None])
    for band_one in range(4):
        real_entries[band_one][band_one] = packed[band_one]
    for number, band_pair in enumerate(BAND_PAIRS):
        upper_band, lower_band = band_pair
        real_entries[upper_band][lower_band] = packed[4 + number]
        real_entries[lower_band][upper_band] = packed[4 + number]
        imaginary_entries[upper_band][lower_band] = packed[10 + number]
        imaginary_entries[lower_band][upper_band] = -packed[10 + number]
    return (real_entries, imaginary_entries)


def product_sum(terms):
    summed = None
    for factor, left_value, right_value in terms:
        if left_value is None or right_value is None:
            continue
        product = factor * left_value * right_value
        summed = product if summed is None else summed + product
    return summed


def commutator(coupled, packed_state_matrix):
    coupled_real, coupled_imaginary = unpack(coupled)
    state_real, state_imaginary = unpack(packed_state_matrix)

    def element(row_band, column_band):
        real_terms = []
        imaginary_terms = []
        for middle in range(4):
            real_terms.append(
                (1.0, coupled_real[row_band][middle], state_real[middle][column_band])
            )
            real_terms.append(
                (-1.0, coupled_imaginary[row_band][middle], state_imaginary[middle][column_band])
            )
            real_terms.append(
                (-1.0, state_real[row_band][middle], coupled_real[middle][column_band])
            )
            real_terms.append(
                (1.0, state_imaginary[row_band][middle], coupled_imaginary[middle][column_band])
            )
            imaginary_terms.append(
                (1.0, coupled_real[row_band][middle], state_imaginary[middle][column_band])
            )
            imaginary_terms.append(
                (1.0, coupled_imaginary[row_band][middle], state_real[middle][column_band])
            )
            imaginary_terms.append(
                (-1.0, state_real[row_band][middle], coupled_imaginary[middle][column_band])
            )
            imaginary_terms.append(
                (-1.0, state_imaginary[row_band][middle], coupled_real[middle][column_band])
            )
        return (product_sum(real_terms), product_sum(imaginary_terms))

    diagonal = []
    upper_real = []
    upper_imaginary = []
    for band_one in range(4):
        diagonal.append(element(band_one, band_one)[1])
    for upper_band, lower_band in BAND_PAIRS:
        real_value, imaginary_value = element(upper_band, lower_band)
        upper_real.append(imaginary_value)
        upper_imaginary.append(-real_value)
    return jnp.stack(diagonal + upper_real + upper_imaginary)


def slope_terms(
    packed_state_matrix,
    energies,
    self_energy,
    gradient_x,
    gradient_y,
    dipole_x,
    dipole_y,
    driving_field,
):
    field_x = driving_field[0]
    field_y = driving_field[1]
    coupled = jnp.concatenate(
        [energies + self_energy[0:4], self_energy[4:16] + field_x * dipole_x + field_y * dipole_y]
    )
    rotation = commutator(coupled, packed_state_matrix)
    drift = rotation + field_x * gradient_x + field_y * gradient_y
    return jnp.concatenate([drift[0:4], drift[4:16] - DEPHASING * packed_state_matrix[4:16]])


def contract(einsum_form, left, right):
    return jnp.einsum(
        einsum_form, left, right, precision=lax.Precision.HIGHEST, preferred_element_type=jnp.float32
    )


def angles(row_count, column_count, period):
    row_index = np.arange(row_count, dtype=np.int64)[:, None]
    column_index = np.arange(column_count, dtype=np.int64)[None, :]
    return (row_index * column_index % period).astype(np.float64) * (2.0 * math.pi / period)


def table(values):
    return jnp.asarray(values.astype(np.float32))


def hartley_tables(x_length, groups, group_length):
    x_angle = angles(x_length, x_length, x_length)
    group_angle = angles(groups, groups, groups)
    twist_angle = angles(groups, group_length, groups * group_length)
    inner_angle = angles(group_length, group_length, group_length)
    return dict(
        cas_x=table(np.cos(x_angle) + np.sin(x_angle)),
        group_cos=table(np.cos(group_angle)),
        group_sin=table(np.sin(group_angle)),
        twist_cos=table(np.cos(twist_angle)[None, :, None, :]),
        twist_sin=table(np.sin(twist_angle)[None, :, None, :]),
        inner_plus=table(np.cos(inner_angle) + np.sin(inner_angle)),
        inner_minus=table(np.cos(inner_angle) - np.sin(inner_angle)),
    )


def hartley_y(data, tables):
    first_real = contract("ka,capb->ckpb", tables["group_cos"], data)
    first_imaginary = -contract("ka,capb->ckpb", tables["group_sin"], data)
    turned_real = first_real * tables["twist_cos"] + first_imaginary * tables["twist_sin"]
    turned_imaginary = first_imaginary * tables["twist_cos"] - first_real * tables["twist_sin"]
    return contract("ckpb,bq->ckpq", turned_real, tables["inner_plus"]) - contract(
        "ckpb,bq->ckpq", turned_imaginary, tables["inner_minus"]
    )


def hartley_y_transposed(data, tables):
    turned_real = contract("ckpq,bq->ckpb", data, tables["inner_plus"])
    turned_imaginary = -contract("ckpq,bq->ckpb", data, tables["inner_minus"])
    first_real = turned_real * tables["twist_cos"] - turned_imaginary * tables["twist_sin"]
    first_imaginary = turned_real * tables["twist_sin"] + turned_imaginary * tables["twist_cos"]
    return contract("ka,ckpb->capb", tables["group_cos"], first_real) - contract(
        "ka,ckpb->capb", tables["group_sin"], first_imaginary
    )


def with_sums(data, sums, dim):
    shape = list(data.shape)
    shape[dim] = 1
    row = jnp.zeros((1, data.shape[-1]), jnp.float32).at[0, 0 : sums.shape[0]].set(sums)
    return jnp.concatenate([data, jnp.broadcast_to(row.reshape([1] * (data.ndim - 2) + [1, -1]), shape)], axis=dim)


def convolve_and_sum(source, interaction, local_sums, after_transform, primitive_tile_total):
    kx_devices = lax.axis_size("kx")
    ky_devices = lax.axis_size("ky")
    sum_count = 3
    along_kx = lax.all_to_all(source, "kx", split_axis=0, concat_axis=1, tiled=True)
    components, x_length, column_count = along_kx.shape
    row_count = x_length // ky_devices
    tables = hartley_tables(x_length, ky_devices, column_count)
    rows_x = contract("px,cxy->cpy", tables["cas_x"], along_kx)
    rows_x = after_transform(rows_x)
    split = rows_x.reshape(components, ky_devices, row_count, column_count)
    along_ky = lax.all_to_all(split, "ky", split_axis=1, concat_axis=1, tiled=True)
    spectrum = hartley_y(along_ky, tables)
    weight = interaction.reshape(row_count, column_count, ky_devices).transpose(2, 0, 1)
    weighted = spectrum * (weight * (1.0 / primitive_tile_total))[None]
    back_y = with_sums(hartley_y_transposed(weighted, tables), local_sums(), 2)
    returned = lax.all_to_all(back_y, "ky", split_axis=1, concat_axis=1, tiled=True)
    ky_sums = jnp.sum(returned[0, :, row_count, 0:sum_count], axis=0)
    returned = returned[:, :, 0:row_count].reshape(components, x_length, column_count)
    final = contract("px,cpy->cxy", tables["cas_x"], returned)
    rows_local = x_length // kx_devices
    final = with_sums(final.reshape(components, kx_devices, rows_local, column_count), ky_sums, 2)
    back = lax.all_to_all(final, "kx", split_axis=1, concat_axis=0, tiled=True)
    totals = jnp.sum(back[::components, 0, rows_local, 0:sum_count], axis=0) / primitive_tile_total
    convolved = back[:, 0, 0:rows_local].reshape(components * kx_devices, rows_local, column_count)
    return convolved, totals


def neighbours(array, axis, dim, width):
    devices, length = (lax.axis_size(axis), array.shape[dim])
    up = [(i, (i + 1) % devices) for i in range(devices)]
    down = [(j, i) for i, j in up]
    last = lax.slice_in_dim(array, length - width, length, axis=dim)
    initial = lax.slice_in_dim(array, 0, width, axis=dim)
    dense = (-1, 128) if last.size % 128 == 0 else last.shape
    before = lax.ppermute(last.reshape(dense), axis, up).reshape(last.shape)
    after = lax.ppermute(initial.reshape(dense), axis, down).reshape(initial.shape)
    return jnp.concatenate([before, array, after], axis=dim)


def body(packed_state_matrix, energies, dipole_x, dipole_y, interaction, driving_field):
    rows_local = packed_state_matrix.shape[1]
    columns_local = packed_state_matrix.shape[2]
    primitive_tile_total = rows_local * columns_local * lax.axis_size("kx") * lax.axis_size("ky")
    populations = packed_state_matrix[0:4]
    halo_source = []
    gradients = []

    def after_transform(rows_x):
        rows_x, late = lax.optimization_barrier((rows_x, jnp.concatenate([packed_state_matrix, energies])))
        halo_source.append(late)
        return rows_x

    def local_sums():
        stacked = halo_source[0]
        column_core = neighbours(stacked, "kx", 1, 2)
        row_core = neighbours(stacked, "ky", 2, 2)
        gradient_x = (
            8.0 * (column_core[:, 3:-1] - column_core[:, 1:-3])
            - (column_core[:, 4:] - column_core[:, :-4])
        ) / 12.0
        gradient_y = (
            8.0 * (row_core[:, :, 3:-1] - row_core[:, :, 1:-3])
            - (row_core[:, :, 4:] - row_core[:, :, :-4])
        ) / 12.0
        gradients.extend([gradient_x, gradient_y])
        return jnp.stack(
            [
                jnp.sum(packed_state_matrix[2] + packed_state_matrix[3]),
                jnp.sum(gradient_x[16:20] * populations),
                jnp.sum(gradient_y[16:20] * populations),
            ]
        )

    convolved, totals = convolve_and_sum(
        packed_state_matrix, interaction, local_sums, after_transform, primitive_tile_total
    )
    gradient_x, gradient_y = gradients
    shielding_multiplier = 1.0 / (1.0 + SHIELDING_LEVEL * totals[0])
    self_energy = -shielding_multiplier * convolved
    section_slope = slope_terms(
        packed_state_matrix,
        energies,
        self_energy,
        gradient_x[0:16],
        gradient_y[0:16],
        dipole_x,
        dipole_y,
        driving_field,
    )
    field_next = driving_field - COUPLING * totals[1:3]
    return (section_slope, field_next)


def solution(mesh):
    in_specs = (
        P(None, "kx", "ky"),
        P(None, "kx", "ky"),
        P(None, "kx", "ky"),
        P(None, "kx", "ky"),
        P("ky", None),
        P(),
    )
    out_specs = (P(None, "kx", "ky"), P())
    return jax.shard_map(body, mesh=mesh, in_specs=in_specs, out_specs=out_specs, check_vma=False)
```

```python
import math

import jax
import numpy as np
import jax.numpy as jnp
from jax import lax
from jax.sharding import PartitionSpec as P

BAND_PAIRS = ((0, 1), (0, 2), (0, 3), (1, 2), (1, 3), (2, 3))
DEPHASING = 0.5
SHIELDING_LEVEL = 2.0
COUPLING = 40.0


def unpack(packed):
    real_entries = []
    imaginary_entries = []
    for band_one in range(4):
        real_entries.append([None, None, None, None])
        imaginary_entries.append([None, None, None, None])
    for band_one in range(4):
        real_entries[band_one][band_one] = packed[band_one]
    for number, band_pair in enumerate(BAND_PAIRS):
        upper_band, lower_band = band_pair
        real_entries[upper_band][lower_band] = packed[4 + number]
        real_entries[lower_band][upper_band] = packed[4 + number]
        imaginary_entries[upper_band][lower_band] = packed[10 + number]
        imaginary_entries[lower_band][upper_band] = -packed[10 + number]
    return (real_entries, imaginary_entries)


def product_sum(terms):
    summed = None
    for factor, left_value, right_value in terms:
        if left_value is None or right_value is None:
            continue
        product = factor * left_value * right_value
        summed = product if summed is None else summed + product
    return summed


def commutator(coupled, packed_state_matrix):
    coupled_real, coupled_imaginary = unpack(coupled)
    state_real, state_imaginary = unpack(packed_state_matrix)

    def element(row_band, column_band):
        real_terms = []
        imaginary_terms = []
        for middle in range(4):
            real_terms.append(
                (1.0, coupled_real[row_band][middle], state_real[middle][column_band])
            )
            real_terms.append(
                (-1.0, coupled_imaginary[row_band][middle], state_imaginary[middle][column_band])
            )
            real_terms.append(
                (-1.0, state_real[row_band][middle], coupled_real[middle][column_band])
            )
            real_terms.append(
                (1.0, state_imaginary[row_band][middle], coupled_imaginary[middle][column_band])
            )
            imaginary_terms.append(
                (1.0, coupled_real[row_band][middle], state_imaginary[middle][column_band])
            )
            imaginary_terms.append(
                (1.0, coupled_imaginary[row_band][middle], state_real[middle][column_band])
            )
            imaginary_terms.append(
                (-1.0, state_real[row_band][middle], coupled_imaginary[middle][column_band])
            )
            imaginary_terms.append(
                (-1.0, state_imaginary[row_band][middle], coupled_real[middle][column_band])
            )
        return (product_sum(real_terms), product_sum(imaginary_terms))

    diagonal = []
    upper_real = []
    upper_imaginary = []
    for band_one in range(4):
        diagonal.append(element(band_one, band_one)[1])
    for upper_band, lower_band in BAND_PAIRS:
        real_value, imaginary_value = element(upper_band, lower_band)
        upper_real.append(imaginary_value)
        upper_imaginary.append(-real_value)
    return jnp.stack(diagonal + upper_real + upper_imaginary)


def slope_terms(
    packed_state_matrix,
    energies,
    self_energy,
    gradient_x,
    gradient_y,
    dipole_x,
    dipole_y,
    driving_field,
):
    field_x = driving_field[0]
    field_y = driving_field[1]
    coupled = jnp.concatenate(
        [energies + self_energy[0:4], self_energy[4:16] + field_x * dipole_x + field_y * dipole_y]
    )
    rotation = commutator(coupled, packed_state_matrix)
    drift = rotation + field_x * gradient_x + field_y * gradient_y
    return jnp.concatenate([drift[0:4], drift[4:16] - DEPHASING * packed_state_matrix[4:16]])


def contract(einsum_form, left, right):
    return jnp.einsum(
        einsum_form, left, right, precision=lax.Precision.HIGHEST, preferred_element_type=jnp.float32
    )


def angles(row_count, column_count, period):
    row_index = np.arange(row_count, dtype=np.int64)[:, None]
    column_index = np.arange(column_count, dtype=np.int64)[None, :]
    return (row_index * column_index % period).astype(np.float64) * (2.0 * math.pi / period)


def table(values):
    return jnp.asarray(values.astype(np.float32))


def hartley_tables(x_length, groups, group_length):
    x_angle = angles(x_length, x_length, x_length)
    group_angle = angles(groups, groups, groups)
    twist_angle = angles(groups, group_length, groups * group_length)
    inner_angle = angles(group_length, group_length, group_length)
    return dict(
        cas_x=table(np.cos(x_angle) + np.sin(x_angle)),
        group_cos=table(np.cos(group_angle)),
        group_sin=table(np.sin(group_angle)),
        twist_cos=table(np.cos(twist_angle)[None, :, None, :]),
        twist_sin=table(np.sin(twist_angle)[None, :, None, :]),
        inner_plus=table(np.cos(inner_angle) + np.sin(inner_angle)),
        inner_minus=table(np.cos(inner_angle) - np.sin(inner_angle)),
    )


def hartley_y(data, tables):
    first_real = contract("ka,capb->ckpb", tables["group_cos"], data)
    first_imaginary = -contract("ka,capb->ckpb", tables["group_sin"], data)
    turned_real = first_real * tables["twist_cos"] + first_imaginary * tables["twist_sin"]
    turned_imaginary = first_imaginary * tables["twist_cos"] - first_real * tables["twist_sin"]
    return contract("ckpb,bq->ckpq", turned_real, tables["inner_plus"]) - contract(
        "ckpb,bq->ckpq", turned_imaginary, tables["inner_minus"]
    )


def hartley_y_transposed(data, tables):
    turned_real = contract("ckpq,bq->ckpb", data, tables["inner_plus"])
    turned_imaginary = -contract("ckpq,bq->ckpb", data, tables["inner_minus"])
    first_real = turned_real * tables["twist_cos"] - turned_imaginary * tables["twist_sin"]
    first_imaginary = turned_real * tables["twist_sin"] + turned_imaginary * tables["twist_cos"]
    return contract("ka,ckpb->capb", tables["group_cos"], first_real) - contract(
        "ka,ckpb->capb", tables["group_sin"], first_imaginary
    )


def with_sums(data, sums, dim):
    shape = list(data.shape)
    shape[dim] = 1
    row = jnp.zeros((1, data.shape[-1]), jnp.float32).at[0, 0 : sums.shape[0]].set(sums)
    return jnp.concatenate([data, jnp.broadcast_to(row.reshape([1] * (data.ndim - 2) + [1, -1]), shape)], axis=dim)


def convolve_and_sum(source, interaction, local_sums, after_transform, primitive_tile_total):
    kx_devices = lax.axis_size("kx")
    ky_devices = lax.axis_size("ky")
    sum_count = 3
    along_kx = lax.all_to_all(source, "kx", split_axis=0, concat_axis=1, tiled=True)
    components, x_length, column_count = along_kx.shape
    row_count = x_length // ky_devices
    tables = hartley_tables(x_length, ky_devices, column_count)
    rows_x = contract("px,cxy->cpy", tables["cas_x"], along_kx)
    rows_x = after_transform(rows_x)
    split = rows_x.reshape(components, ky_devices, row_count, column_count)
    along_ky = lax.all_to_all(split, "ky", split_axis=1, concat_axis=1, tiled=True)
    spectrum = hartley_y(along_ky, tables)
    weight = interaction.reshape(row_count, column_count, ky_devices).transpose(2, 0, 1)
    weighted = spectrum * (weight * (1.0 / primitive_tile_total))[None]
    back_y = with_sums(hartley_y_transposed(weighted, tables), local_sums(), 2)
    returned = lax.all_to_all(back_y, "ky", split_axis=1, concat_axis=1, tiled=True)
    ky_sums = jnp.sum(returned[0, :, row_count, 0:sum_count], axis=0)
    returned = returned[:, :, 0:row_count].reshape(components, x_length, column_count)
    final = contract("px,cpy->cxy", tables["cas_x"], returned)
    rows_local = x_length // kx_devices
    final = with_sums(final.reshape(components, kx_devices, rows_local, column_count), ky_sums, 2)
    back = lax.all_to_all(final, "kx", split_axis=1, concat_axis=0, tiled=True)
    totals = jnp.sum(back[::components, 0, rows_local, 0:sum_count], axis=0) / primitive_tile_total
    convolved = back[:, 0, 0:rows_local].reshape(components * kx_devices, rows_local, column_count)
    return convolved, totals


def neighbours(array, axis, dim, width):
    devices, length = (lax.axis_size(axis), array.shape[dim])
    up = [(i, (i + 1) % devices) for i in range(devices)]
    down = [(j, i) for i, j in up]
    last = lax.slice_in_dim(array, length - width, length, axis=dim)
    initial = lax.slice_in_dim(array, 0, width, axis=dim)
    dense = (-1, 128) if last.size % 128 == 0 else last.shape
    before = lax.ppermute(last.reshape(dense), axis, up).reshape(last.shape)
    after = lax.ppermute(initial.reshape(dense), axis, down).reshape(initial.shape)
    return jnp.concatenate([before, array, after], axis=dim)


def body(packed_state_matrix, energies, dipole_x, dipole_y, interaction, driving_field):
    rows_local = packed_state_matrix.shape[1]
    columns_local = packed_state_matrix.shape[2]
    primitive_tile_total = rows_local * columns_local * lax.axis_size("kx") * lax.axis_size("ky")
    populations = packed_state_matrix[0:4]
    halo_source = []
    gradients = []

    def after_transform(rows_x):
        rows_x, late = lax.optimization_barrier((rows_x, jnp.concatenate([packed_state_matrix, energies])))
        halo_source.append(late)
        return rows_x

    def local_sums():
        column_core = neighbours(jnp.concatenate([packed_state_matrix, energies]), "kx", 1, 2)
        row_core = neighbours(halo_source[0], "ky", 2, 2)
        gradient_x = (
            8.0 * (column_core[:, 3:-1] - column_core[:, 1:-3])
            - (column_core[:, 4:] - column_core[:, :-4])
        ) / 12.0
        gradient_y = (
            8.0 * (row_core[:, :, 3:-1] - row_core[:, :, 1:-3])
            - (row_core[:, :, 4:] - row_core[:, :, :-4])
        ) / 12.0
        gradients.extend([gradient_x, gradient_y])
        return jnp.stack(
            [
                jnp.sum(packed_state_matrix[2] + packed_state_matrix[3]),
                jnp.sum(gradient_x[16:20] * populations),
                jnp.sum(gradient_y[16:20] * populations),
            ]
        )

    convolved, totals = convolve_and_sum(
        packed_state_matrix, interaction, local_sums, after_transform, primitive_tile_total
    )
    gradient_x, gradient_y = gradients
    shielding_multiplier = 1.0 / (1.0 + SHIELDING_LEVEL * totals[0])
    self_energy = -shielding_multiplier * convolved
    section_slope = slope_terms(
        packed_state_matrix,
        energies,
        self_energy,
        gradient_x[0:16],
        gradient_y[0:16],
        dipole_x,
        dipole_y,
        driving_field,
    )
    field_next = driving_field - COUPLING * totals[1:3]
    return (section_slope, field_next)


def solution(mesh):
    in_specs = (
        P(None, "kx", "ky"),
        P(None, "kx", "ky"),
        P(None, "kx", "ky"),
        P(None, "kx", "ky"),
        P("ky", None),
        P(),
    )
    out_specs = (P(None, "kx", "ky"), P())
    return jax.shard_map(body, mesh=mesh, in_specs=in_specs, out_specs=out_specs, check_vma=False)
```

```python
import math

import jax
import numpy as np
import jax.numpy as jnp
from jax import lax
from jax.sharding import PartitionSpec as P

BAND_PAIRS = ((0, 1), (0, 2), (0, 3), (1, 2), (1, 3), (2, 3))
DEPHASING = 0.5
SHIELDING_LEVEL = 2.0
COUPLING = 40.0
KY = ("kz", "kh")


def unpack(packed):
    real_entries = []
    imaginary_entries = []
    for band_one in range(4):
        real_entries.append([None, None, None, None])
        imaginary_entries.append([None, None, None, None])
    for band_one in range(4):
        real_entries[band_one][band_one] = packed[band_one]
    for number, band_pair in enumerate(BAND_PAIRS):
        upper_band, lower_band = band_pair
        real_entries[upper_band][lower_band] = packed[4 + number]
        real_entries[lower_band][upper_band] = packed[4 + number]
        imaginary_entries[upper_band][lower_band] = packed[10 + number]
        imaginary_entries[lower_band][upper_band] = -packed[10 + number]
    return (real_entries, imaginary_entries)


def product_sum(terms):
    summed = None
    for factor, left_value, right_value in terms:
        if left_value is None or right_value is None:
            continue
        product = factor * left_value * right_value
        summed = product if summed is None else summed + product
    return summed


def commutator(coupled, packed_state_matrix):
    coupled_real, coupled_imaginary = unpack(coupled)
    state_real, state_imaginary = unpack(packed_state_matrix)

    def element(row_band, column_band):
        real_terms = []
        imaginary_terms = []
        for middle in range(4):
            real_terms.append(
                (1.0, coupled_real[row_band][middle], state_real[middle][column_band])
            )
            real_terms.append(
                (-1.0, coupled_imaginary[row_band][middle], state_imaginary[middle][column_band])
            )
            real_terms.append(
                (-1.0, state_real[row_band][middle], coupled_real[middle][column_band])
            )
            real_terms.append(
                (1.0, state_imaginary[row_band][middle], coupled_imaginary[middle][column_band])
            )
            imaginary_terms.append(
                (1.0, coupled_real[row_band][middle], state_imaginary[middle][column_band])
            )
            imaginary_terms.append(
                (1.0, coupled_imaginary[row_band][middle], state_real[middle][column_band])
            )
            imaginary_terms.append(
                (-1.0, state_real[row_band][middle], coupled_imaginary[middle][column_band])
            )
            imaginary_terms.append(
                (-1.0, state_imaginary[row_band][middle], coupled_real[middle][column_band])
            )
        return (product_sum(real_terms), product_sum(imaginary_terms))

    diagonal = []
    upper_real = []
    upper_imaginary = []
    for band_one in range(4):
        diagonal.append(element(band_one, band_one)[1])
    for upper_band, lower_band in BAND_PAIRS:
        real_value, imaginary_value = element(upper_band, lower_band)
        upper_real.append(imaginary_value)
        upper_imaginary.append(-real_value)
    return jnp.stack(diagonal + upper_real + upper_imaginary)


def slope_terms(
    packed_state_matrix,
    energies,
    self_energy,
    gradient_x,
    gradient_y,
    dipole_x,
    dipole_y,
    driving_field,
):
    field_x = driving_field[0]
    field_y = driving_field[1]
    coupled = jnp.concatenate(
        [energies + self_energy[0:4], self_energy[4:16] + field_x * dipole_x + field_y * dipole_y]
    )
    rotation = commutator(coupled, packed_state_matrix)
    drift = rotation + field_x * gradient_x + field_y * gradient_y
    return jnp.concatenate([drift[0:4], drift[4:16] - DEPHASING * packed_state_matrix[4:16]])


def contract(einsum_form, left, right):
    return jnp.einsum(
        einsum_form, left, right, precision=lax.Precision.HIGHEST, preferred_element_type=jnp.float32
    )


def angles(row_count, column_count, period):
    row_index = np.arange(row_count, dtype=np.int64)[:, None]
    column_index = np.arange(column_count, dtype=np.int64)[None, :]
    return (row_index * column_index % period).astype(np.float64) * (2.0 * math.pi / period)


def table(values):
    return jnp.asarray(values.astype(np.float32))


def hartley_tables(x_length, groups, group_length):
    x_angle = angles(x_length, x_length, x_length)
    group_angle = angles(groups, groups, groups)
    twist_angle = angles(groups, group_length, groups * group_length)
    inner_angle = angles(group_length, group_length, group_length)
    return dict(
        cas_x=table(np.cos(x_angle) + np.sin(x_angle)),
        group_cos=table(np.cos(group_angle)),
        group_sin=table(np.sin(group_angle)),
        twist_cos=table(np.cos(twist_angle)[None, :, None, :]),
        twist_sin=table(np.sin(twist_angle)[None, :, None, :]),
        inner_plus=table(np.cos(inner_angle) + np.sin(inner_angle)),
        inner_minus=table(np.cos(inner_angle) - np.sin(inner_angle)),
    )


def hartley_y(data, tables):
    first_real = contract("ka,capb->ckpb", tables["group_cos"], data)
    first_imaginary = -contract("ka,capb->ckpb", tables["group_sin"], data)
    turned_real = first_real * tables["twist_cos"] + first_imaginary * tables["twist_sin"]
    turned_imaginary = first_imaginary * tables["twist_cos"] - first_real * tables["twist_sin"]
    return contract("ckpb,bq->ckpq", turned_real, tables["inner_plus"]) - contract(
        "ckpb,bq->ckpq", turned_imaginary, tables["inner_minus"]
    )


def hartley_y_transposed(data, tables):
    turned_real = contract("ckpq,bq->ckpb", data, tables["inner_plus"])
    turned_imaginary = -contract("ckpq,bq->ckpb", data, tables["inner_minus"])
    first_real = turned_real * tables["twist_cos"] - turned_imaginary * tables["twist_sin"]
    first_imaginary = turned_real * tables["twist_sin"] + turned_imaginary * tables["twist_cos"]
    return contract("ka,ckpb->capb", tables["group_cos"], first_real) - contract(
        "ka,ckpb->capb", tables["group_sin"], first_imaginary
    )


def with_sums(data, sums, dim):
    shape = list(data.shape)
    shape[dim] = 1
    row = jnp.zeros((1, data.shape[-1]), jnp.float32).at[0, 0 : sums.shape[0]].set(sums)
    return jnp.concatenate([data, jnp.broadcast_to(row.reshape([1] * (data.ndim - 2) + [1, -1]), shape)], axis=dim)


def ky_exchange(data, order):
    shape = data.shape
    split = data.reshape(shape[0], lax.axis_size("kz"), lax.axis_size("kh"), *shape[2:])
    for axis in order:
        dim = 1 if axis == "kz" else 2
        split = lax.all_to_all(split, axis, split_axis=dim, concat_axis=dim, tiled=True)
    return split.reshape(shape)


def convolve_and_sum(source, interaction, local_sums, after_transform, primitive_tile_total):
    kx_devices = lax.axis_size("kx")
    ky_devices = lax.axis_size(KY)
    sum_count = 3
    along_kx = lax.all_to_all(source, "kx", split_axis=0, concat_axis=1, tiled=True)
    components, x_length, column_count = along_kx.shape
    row_count = x_length // ky_devices
    tables = hartley_tables(x_length, ky_devices, column_count)
    rows_x = contract("px,cxy->cpy", tables["cas_x"], along_kx)
    rows_x = after_transform(rows_x)
    split = rows_x.reshape(components, ky_devices, row_count, column_count)
    along_ky = ky_exchange(split, ("kh", "kz"))
    spectrum = hartley_y(along_ky, tables)
    weight = interaction.reshape(row_count, column_count, ky_devices).transpose(2, 0, 1)
    weighted = spectrum * (weight * (1.0 / primitive_tile_total))[None]
    back_y = with_sums(hartley_y_transposed(weighted, tables), local_sums(), 2)
    returned = ky_exchange(back_y, ("kz", "kh"))
    ky_sums = jnp.sum(returned[0, :, row_count, 0:sum_count], axis=0)
    returned = returned[:, :, 0:row_count].reshape(components, x_length, column_count)
    final = contract("px,cpy->cxy", tables["cas_x"], returned)
    rows_local = x_length // kx_devices
    final = with_sums(final.reshape(components, kx_devices, rows_local, column_count), ky_sums, 2)
    back = lax.all_to_all(final, "kx", split_axis=1, concat_axis=0, tiled=True)
    totals = jnp.sum(back[::components, 0, rows_local, 0:sum_count], axis=0) / primitive_tile_total
    convolved = back[:, 0, 0:rows_local].reshape(components * kx_devices, rows_local, column_count)
    return convolved, totals


def neighbours(array, axis, dim, width):
    devices, length = (lax.axis_size(axis), array.shape[dim])
    up = [(i, (i + 1) % devices) for i in range(devices)]
    down = [(j, i) for i, j in up]
    last = lax.slice_in_dim(array, length - width, length, axis=dim)
    initial = lax.slice_in_dim(array, 0, width, axis=dim)
    dense = (-1, 128) if last.size % 128 == 0 else last.shape
    before = lax.ppermute(last.reshape(dense), axis, up).reshape(last.shape)
    after = lax.ppermute(initial.reshape(dense), axis, down).reshape(initial.shape)
    return jnp.concatenate([before, array, after], axis=dim)


def body(packed_state_matrix, energies, dipole_x, dipole_y, interaction, driving_field):
    rows_local = packed_state_matrix.shape[1]
    columns_local = packed_state_matrix.shape[2]
    primitive_tile_total = rows_local * columns_local * lax.axis_size("kx") * lax.axis_size(KY)
    populations = packed_state_matrix[0:4]
    halo_source = []
    gradients = []

    def after_transform(rows_x):
        rows_x, late = lax.optimization_barrier((rows_x, jnp.concatenate([packed_state_matrix, energies])))
        halo_source.append(late)
        return rows_x

    def local_sums():
        column_core = neighbours(jnp.concatenate([packed_state_matrix, energies]), "kx", 1, 2)
        row_core = neighbours(halo_source[0], KY, 2, 2)
        gradient_x = (
            8.0 * (column_core[:, 3:-1] - column_core[:, 1:-3])
            - (column_core[:, 4:] - column_core[:, :-4])
        ) / 12.0
        gradient_y = (
            8.0 * (row_core[:, :, 3:-1] - row_core[:, :, 1:-3])
            - (row_core[:, :, 4:] - row_core[:, :, :-4])
        ) / 12.0
        gradients.extend([gradient_x, gradient_y])
        return jnp.stack(
            [
                jnp.sum(packed_state_matrix[2] + packed_state_matrix[3]),
                jnp.sum(gradient_x[16:20] * populations),
                jnp.sum(gradient_y[16:20] * populations),
            ]
        )

    convolved, totals = convolve_and_sum(
        packed_state_matrix, interaction, local_sums, after_transform, primitive_tile_total
    )
    gradient_x, gradient_y = gradients
    shielding_multiplier = 1.0 / (1.0 + SHIELDING_LEVEL * totals[0])
    self_energy = -shielding_multiplier * convolved
    section_slope = slope_terms(
        packed_state_matrix,
        energies,
        self_energy,
        gradient_x[0:16],
        gradient_y[0:16],
        dipole_x,
        dipole_y,
        driving_field,
    )
    field_next = driving_field - COUPLING * totals[1:3]
    return (section_slope, field_next)


def solution(mesh):
    kx_size, ky_size = mesh.devices.shape
    split_mesh = jax.sharding.Mesh(
        mesh.devices.reshape(kx_size, ky_size // 2, 2), ("kx", "kz", "kh")
    )
    in_specs = (
        P(None, "kx", KY),
        P(None, "kx", KY),
        P(None, "kx", KY),
        P(None, "kx", KY),
        P(KY, None),
        P(),
    )
    out_specs = (P(None, "kx", KY), P())
    return jax.shard_map(body, mesh=split_mesh, in_specs=in_specs, out_specs=out_specs, check_vma=False)
```

```python
import math

import jax
import numpy as np
import jax.numpy as jnp
from jax import lax
from jax.sharding import PartitionSpec as P

BAND_PAIRS = ((0, 1), (0, 2), (0, 3), (1, 2), (1, 3), (2, 3))
DEPHASING = 0.5
SHIELDING_LEVEL = 2.0
COUPLING = 40.0


def unpack(packed):
    real_entries = []
    imaginary_entries = []
    for band_one in range(4):
        real_entries.append([None, None, None, None])
        imaginary_entries.append([None, None, None, None])
    for band_one in range(4):
        real_entries[band_one][band_one] = packed[band_one]
    for number, band_pair in enumerate(BAND_PAIRS):
        upper_band, lower_band = band_pair
        real_entries[upper_band][lower_band] = packed[4 + number]
        real_entries[lower_band][upper_band] = packed[4 + number]
        imaginary_entries[upper_band][lower_band] = packed[10 + number]
        imaginary_entries[lower_band][upper_band] = -packed[10 + number]
    return (real_entries, imaginary_entries)


def product_sum(terms):
    summed = None
    for factor, left_value, right_value in terms:
        if left_value is None or right_value is None:
            continue
        product = factor * left_value * right_value
        summed = product if summed is None else summed + product
    return summed


def commutator(coupled, packed_state_matrix):
    coupled_real, coupled_imaginary = unpack(coupled)
    state_real, state_imaginary = unpack(packed_state_matrix)

    def element(row_band, column_band):
        real_terms = []
        imaginary_terms = []
        for middle in range(4):
            real_terms.append(
                (1.0, coupled_real[row_band][middle], state_real[middle][column_band])
            )
            real_terms.append(
                (-1.0, coupled_imaginary[row_band][middle], state_imaginary[middle][column_band])
            )
            real_terms.append(
                (-1.0, state_real[row_band][middle], coupled_real[middle][column_band])
            )
            real_terms.append(
                (1.0, state_imaginary[row_band][middle], coupled_imaginary[middle][column_band])
            )
            imaginary_terms.append(
                (1.0, coupled_real[row_band][middle], state_imaginary[middle][column_band])
            )
            imaginary_terms.append(
                (1.0, coupled_imaginary[row_band][middle], state_real[middle][column_band])
            )
            imaginary_terms.append(
                (-1.0, state_real[row_band][middle], coupled_imaginary[middle][column_band])
            )
            imaginary_terms.append(
                (-1.0, state_imaginary[row_band][middle], coupled_real[middle][column_band])
            )
        return (product_sum(real_terms), product_sum(imaginary_terms))

    diagonal = []
    upper_real = []
    upper_imaginary = []
    for band_one in range(4):
        diagonal.append(element(band_one, band_one)[1])
    for upper_band, lower_band in BAND_PAIRS:
        real_value, imaginary_value = element(upper_band, lower_band)
        upper_real.append(imaginary_value)
        upper_imaginary.append(-real_value)
    return jnp.stack(diagonal + upper_real + upper_imaginary)


def slope_terms(
    packed_state_matrix,
    energies,
    self_energy,
    gradient_x,
    gradient_y,
    dipole_x,
    dipole_y,
    driving_field,
):
    field_x = driving_field[0]
    field_y = driving_field[1]
    coupled = jnp.concatenate(
        [energies + self_energy[0:4], self_energy[4:16] + field_x * dipole_x + field_y * dipole_y]
    )
    rotation = commutator(coupled, packed_state_matrix)
    drift = rotation + field_x * gradient_x + field_y * gradient_y
    return jnp.concatenate([drift[0:4], drift[4:16] - DEPHASING * packed_state_matrix[4:16]])


def contract(einsum_form, left, right):
    return jnp.einsum(
        einsum_form, left, right, precision=lax.Precision.HIGHEST, preferred_element_type=jnp.float32
    )


def angles(row_count, column_count, period):
    row_index = np.arange(row_count, dtype=np.int64)[:, None]
    column_index = np.arange(column_count, dtype=np.int64)[None, :]
    return (row_index * column_index % period).astype(np.float64) * (2.0 * math.pi / period)


def table(values):
    return jnp.asarray(values.astype(np.float32))


def hartley_tables(x_length, groups, group_length):
    x_angle = angles(x_length, x_length, x_length)
    group_angle = angles(groups, groups, groups)
    twist_angle = angles(groups, group_length, groups * group_length)
    inner_angle = angles(group_length, group_length, group_length)
    return dict(
        cas_x=table(np.cos(x_angle) + np.sin(x_angle)),
        group=table(np.stack([np.cos(group_angle), -np.sin(group_angle)])),
        twist_cos=table(np.cos(twist_angle)[None, :, None, :]),
        twist_sin=table(np.sin(twist_angle)[None, :, None, :]),
        inner=table(
            np.stack(
                [np.cos(inner_angle) + np.sin(inner_angle), np.sin(inner_angle) - np.cos(inner_angle)]
            )
        ),
    )


def hartley_y(data, tables):
    first_real, first_imaginary = contract("ska,capb->sckpb", tables["group"], data)
    turned_real = first_real * tables["twist_cos"] + first_imaginary * tables["twist_sin"]
    turned_imaginary = first_imaginary * tables["twist_cos"] - first_real * tables["twist_sin"]
    turned = jnp.stack([turned_real, turned_imaginary])
    return contract("sckpb,sbq->ckpq", turned, tables["inner"])


def hartley_y_transposed(data, tables):
    turned_real, turned_imaginary = contract("ckpq,sbq->sckpb", data, tables["inner"])
    first_real = turned_real * tables["twist_cos"] - turned_imaginary * tables["twist_sin"]
    first_imaginary = turned_real * tables["twist_sin"] + turned_imaginary * tables["twist_cos"]
    first = jnp.stack([first_real, first_imaginary])
    return contract("ska,sckpb->capb", tables["group"], first)


def with_sums(data, sums, dim):
    shape = list(data.shape)
    shape[dim] = 1
    row = jnp.zeros((1, data.shape[-1]), jnp.float32).at[0, 0 : sums.shape[0]].set(sums)
    return jnp.concatenate([data, jnp.broadcast_to(row.reshape([1] * (data.ndim - 2) + [1, -1]), shape)], axis=dim)


def convolve_and_sum(source, interaction, local_sums, after_transform, primitive_tile_total):
    kx_devices = lax.axis_size("kx")
    ky_devices = lax.axis_size("ky")
    sum_count = 3
    along_kx = lax.all_to_all(source, "kx", split_axis=0, concat_axis=1, tiled=True)
    components, x_length, column_count = along_kx.shape
    row_count = x_length // ky_devices
    tables = hartley_tables(x_length, ky_devices, column_count)
    rows_x = contract("px,cxy->cpy", tables["cas_x"], along_kx)
    rows_x = after_transform(rows_x)
    split = rows_x.reshape(components, ky_devices, row_count, column_count)
    along_ky = lax.all_to_all(split, "ky", split_axis=1, concat_axis=1, tiled=True)
    spectrum = hartley_y(along_ky, tables)
    weight = interaction.reshape(row_count, column_count, ky_devices).transpose(2, 0, 1)
    weighted = spectrum * (weight * (1.0 / primitive_tile_total))[None]
    back_y = with_sums(hartley_y_transposed(weighted, tables), local_sums(), 2)
    returned = lax.all_to_all(back_y, "ky", split_axis=1, concat_axis=1, tiled=True)
    ky_sums = jnp.sum(returned[0, :, row_count, 0:sum_count], axis=0)
    returned = returned[:, :, 0:row_count].reshape(components, x_length, column_count)
    final = contract("px,cpy->cxy", tables["cas_x"], returned)
    rows_local = x_length // kx_devices
    final = with_sums(final.reshape(components, kx_devices, rows_local, column_count), ky_sums, 2)
    back = lax.all_to_all(final, "kx", split_axis=1, concat_axis=0, tiled=True)
    totals = jnp.sum(back[::components, 0, rows_local, 0:sum_count], axis=0) / primitive_tile_total
    convolved = back[:, 0, 0:rows_local].reshape(components * kx_devices, rows_local, column_count)
    return convolved, totals


def neighbours(array, axis, dim, width):
    devices, length = (lax.axis_size(axis), array.shape[dim])
    up = [(i, (i + 1) % devices) for i in range(devices)]
    down = [(j, i) for i, j in up]
    last = lax.slice_in_dim(array, length - width, length, axis=dim)
    initial = lax.slice_in_dim(array, 0, width, axis=dim)
    dense = (-1, 128) if last.size % 128 == 0 else last.shape
    before = lax.ppermute(last.reshape(dense), axis, up).reshape(last.shape)
    after = lax.ppermute(initial.reshape(dense), axis, down).reshape(initial.shape)
    return jnp.concatenate([before, array, after], axis=dim)


def body(packed_state_matrix, energies, dipole_x, dipole_y, interaction, driving_field):
    rows_local = packed_state_matrix.shape[1]
    columns_local = packed_state_matrix.shape[2]
    primitive_tile_total = rows_local * columns_local * lax.axis_size("kx") * lax.axis_size("ky")
    populations = packed_state_matrix[0:4]
    halo_source = []
    gradients = []

    def after_transform(rows_x):
        rows_x, late = lax.optimization_barrier((rows_x, jnp.concatenate([packed_state_matrix, energies])))
        halo_source.append(late)
        return rows_x

    def local_sums():
        column_core = neighbours(jnp.concatenate([packed_state_matrix, energies]), "kx", 1, 2)
        row_core = neighbours(halo_source[0], "ky", 2, 2)
        gradient_x = (
            8.0 * (column_core[:, 3:-1] - column_core[:, 1:-3])
            - (column_core[:, 4:] - column_core[:, :-4])
        ) / 12.0
        gradient_y = (
            8.0 * (row_core[:, :, 3:-1] - row_core[:, :, 1:-3])
            - (row_core[:, :, 4:] - row_core[:, :, :-4])
        ) / 12.0
        gradients.extend([gradient_x, gradient_y])
        return jnp.stack(
            [
                jnp.sum(packed_state_matrix[2] + packed_state_matrix[3]),
                jnp.sum(gradient_x[16:20] * populations),
                jnp.sum(gradient_y[16:20] * populations),
            ]
        )

    convolved, totals = convolve_and_sum(
        packed_state_matrix, interaction, local_sums, after_transform, primitive_tile_total
    )
    gradient_x, gradient_y = gradients
    shielding_multiplier = 1.0 / (1.0 + SHIELDING_LEVEL * totals[0])
    self_energy = -shielding_multiplier * convolved
    section_slope = slope_terms(
        packed_state_matrix,
        energies,
        self_energy,
        gradient_x[0:16],
        gradient_y[0:16],
        dipole_x,
        dipole_y,
        driving_field,
    )
    field_next = driving_field - COUPLING * totals[1:3]
    return (section_slope, field_next)


def solution(mesh):
    in_specs = (
        P(None, "kx", "ky"),
        P(None, "kx", "ky"),
        P(None, "kx", "ky"),
        P(None, "kx", "ky"),
        P("ky", None),
        P(),
    )
    out_specs = (P(None, "kx", "ky"), P())
    return jax.shard_map(body, mesh=mesh, in_specs=in_specs, out_specs=out_specs, check_vma=False)
```

```python
import math

import jax
import numpy as np
import jax.numpy as jnp
from jax import lax
from jax.sharding import PartitionSpec as P

BAND_PAIRS = ((0, 1), (0, 2), (0, 3), (1, 2), (1, 3), (2, 3))
DEPHASING = 0.5
SHIELDING_LEVEL = 2.0
COUPLING = 40.0


def unpack(packed):
    real_entries = []
    imaginary_entries = []
    for band_one in range(4):
        real_entries.append([None, None, None, None])
        imaginary_entries.append([None, None, None, None])
    for band_one in range(4):
        real_entries[band_one][band_one] = packed[band_one]
    for number, band_pair in enumerate(BAND_PAIRS):
        upper_band, lower_band = band_pair
        real_entries[upper_band][lower_band] = packed[4 + number]
        real_entries[lower_band][upper_band] = packed[4 + number]
        imaginary_entries[upper_band][lower_band] = packed[10 + number]
        imaginary_entries[lower_band][upper_band] = -packed[10 + number]
    return (real_entries, imaginary_entries)


def product_sum(terms):
    summed = None
    for factor, left_value, right_value in terms:
        if left_value is None or right_value is None:
            continue
        product = factor * left_value * right_value
        summed = product if summed is None else summed + product
    return summed


def commutator(coupled, packed_state_matrix):
    coupled_real, coupled_imaginary = unpack(coupled)
    state_real, state_imaginary = unpack(packed_state_matrix)

    def element(row_band, column_band):
        real_terms = []
        imaginary_terms = []
        for middle in range(4):
            real_terms.append(
                (1.0, coupled_real[row_band][middle], state_real[middle][column_band])
            )
            real_terms.append(
                (-1.0, coupled_imaginary[row_band][middle], state_imaginary[middle][column_band])
            )
            real_terms.append(
                (-1.0, state_real[row_band][middle], coupled_real[middle][column_band])
            )
            real_terms.append(
                (1.0, state_imaginary[row_band][middle], coupled_imaginary[middle][column_band])
            )
            imaginary_terms.append(
                (1.0, coupled_real[row_band][middle], state_imaginary[middle][column_band])
            )
            imaginary_terms.append(
                (1.0, coupled_imaginary[row_band][middle], state_real[middle][column_band])
            )
            imaginary_terms.append(
                (-1.0, state_real[row_band][middle], coupled_imaginary[middle][column_band])
            )
            imaginary_terms.append(
                (-1.0, state_imaginary[row_band][middle], coupled_real[middle][column_band])
            )
        return (product_sum(real_terms), product_sum(imaginary_terms))

    diagonal = []
    upper_real = []
    upper_imaginary = []
    for band_one in range(4):
        diagonal.append(element(band_one, band_one)[1])
    for upper_band, lower_band in BAND_PAIRS:
        real_value, imaginary_value = element(upper_band, lower_band)
        upper_real.append(imaginary_value)
        upper_imaginary.append(-real_value)
    return jnp.stack(diagonal + upper_real + upper_imaginary)


def slope_terms(
    packed_state_matrix,
    energies,
    self_energy,
    gradient_x,
    gradient_y,
    dipole_x,
    dipole_y,
    driving_field,
):
    field_x = driving_field[0]
    field_y = driving_field[1]
    coupled = jnp.concatenate(
        [energies + self_energy[0:4], self_energy[4:16] + field_x * dipole_x + field_y * dipole_y]
    )
    rotation = commutator(coupled, packed_state_matrix)
    drift = rotation + field_x * gradient_x + field_y * gradient_y
    return jnp.concatenate([drift[0:4], drift[4:16] - DEPHASING * packed_state_matrix[4:16]])


def contract(einsum_form, left, right):
    return jnp.einsum(
        einsum_form, left, right, precision=lax.Precision.HIGHEST, preferred_element_type=jnp.float32
    )


def angles(row_count, column_count, period):
    row_index = np.arange(row_count, dtype=np.int64)[:, None]
    column_index = np.arange(column_count, dtype=np.int64)[None, :]
    return (row_index * column_index % period).astype(np.float64) * (2.0 * math.pi / period)


def table(values):
    return jnp.asarray(values.astype(np.float32))


def hartley_tables(x_length, groups, group_length):
    x_angle = angles(x_length, x_length, x_length)
    group_angle = angles(groups, groups, groups)
    twist_angle = angles(groups, group_length, groups * group_length)
    inner_angle = angles(group_length, group_length, group_length)
    return dict(
        cas_x=table(np.cos(x_angle) + np.sin(x_angle)),
        group=table(np.stack([np.cos(group_angle), -np.sin(group_angle)])),
        twist_cos=table(np.cos(twist_angle)[None, :, None, :]),
        twist_sin=table(np.sin(twist_angle)[None, :, None, :]),
        inner=table(
            np.stack(
                [np.cos(inner_angle) + np.sin(inner_angle), np.sin(inner_angle) - np.cos(inner_angle)]
            )
        ),
    )


def hartley_y(data, tables):
    first_real, first_imaginary = contract("ska,capb->sckpb", tables["group"], data)
    turned_real = first_real * tables["twist_cos"] + first_imaginary * tables["twist_sin"]
    turned_imaginary = first_imaginary * tables["twist_cos"] - first_real * tables["twist_sin"]
    turned = jnp.stack([turned_real, turned_imaginary])
    return contract("sckpb,sbq->ckpq", turned, tables["inner"])


def hartley_y_transposed(data, tables):
    turned_real, turned_imaginary = contract("ckpq,sbq->sckpb", data, tables["inner"])
    first_real = turned_real * tables["twist_cos"] - turned_imaginary * tables["twist_sin"]
    first_imaginary = turned_real * tables["twist_sin"] + turned_imaginary * tables["twist_cos"]
    first = jnp.stack([first_real, first_imaginary])
    return contract("ska,sckpb->capb", tables["group"], first)


def with_sums(data, sums, dim):
    shape = list(data.shape)
    shape[dim] = 1
    row = jnp.zeros((1, data.shape[-1]), jnp.float32).at[0, 0 : sums.shape[0]].set(sums)
    return jnp.concatenate([data, jnp.broadcast_to(row.reshape([1] * (data.ndim - 2) + [1, -1]), shape)], axis=dim)


def convolve_and_sum(source, interaction, local_sums, primitive_tile_total):
    kx_devices = lax.axis_size("kx")
    ky_devices = lax.axis_size("ky")
    sum_count = 3
    along_kx = lax.all_to_all(source, "kx", split_axis=0, concat_axis=1, tiled=True)
    components, x_length, column_count = along_kx.shape
    row_count = x_length // ky_devices
    tables = hartley_tables(x_length, ky_devices, column_count)
    rows_x = contract("px,cxy->cpy", tables["cas_x"], along_kx)
    split = rows_x.reshape(components, ky_devices, row_count, column_count)
    along_ky = lax.all_to_all(split, "ky", split_axis=1, concat_axis=1, tiled=True)
    spectrum = hartley_y(along_ky, tables)
    weight = interaction.reshape(row_count, column_count, ky_devices).transpose(2, 0, 1)
    weighted = spectrum * (weight * (1.0 / primitive_tile_total))[None]
    back_y = with_sums(hartley_y_transposed(weighted, tables), local_sums(), 2)
    returned = lax.all_to_all(back_y, "ky", split_axis=1, concat_axis=1, tiled=True)
    ky_sums = jnp.sum(returned[0, :, row_count, 0:sum_count], axis=0)
    returned = returned[:, :, 0:row_count].reshape(components, x_length, column_count)
    final = contract("px,cpy->cxy", tables["cas_x"], returned)
    rows_local = x_length // kx_devices
    final = with_sums(final.reshape(components, kx_devices, rows_local, column_count), ky_sums, 2)
    back = lax.all_to_all(final, "kx", split_axis=1, concat_axis=0, tiled=True)
    totals = jnp.sum(back[::components, 0, rows_local, 0:sum_count], axis=0) / primitive_tile_total
    convolved = back[:, 0, 0:rows_local].reshape(components * kx_devices, rows_local, column_count)
    return convolved, totals


def neighbours(array, axis, dim, width):
    devices, length = (lax.axis_size(axis), array.shape[dim])
    up = [(i, (i + 1) % devices) for i in range(devices)]
    down = [(j, i) for i, j in up]
    last = lax.slice_in_dim(array, length - width, length, axis=dim)
    initial = lax.slice_in_dim(array, 0, width, axis=dim)
    dense = (-1, 128) if last.size % 128 == 0 else last.shape
    before = lax.ppermute(last.reshape(dense), axis, up).reshape(last.shape)
    after = lax.ppermute(initial.reshape(dense), axis, down).reshape(initial.shape)
    return jnp.concatenate([before, array, after], axis=dim)


def body(packed_state_matrix, energies, dipole_x, dipole_y, interaction, driving_field):
    rows_local = packed_state_matrix.shape[1]
    columns_local = packed_state_matrix.shape[2]
    primitive_tile_total = rows_local * columns_local * lax.axis_size("kx") * lax.axis_size("ky")
    populations = packed_state_matrix[0:4]
    stacked = jnp.concatenate([packed_state_matrix, energies])
    column_core = neighbours(stacked, "kx", 1, 2)
    row_core = neighbours(stacked, "ky", 2, 2)
    source, column_core, row_core = lax.optimization_barrier((packed_state_matrix, column_core, row_core))
    gradient_x = (
        8.0 * (column_core[:, 3:-1] - column_core[:, 1:-3])
        - (column_core[:, 4:] - column_core[:, :-4])
    ) / 12.0
    gradient_y = (
        8.0 * (row_core[:, :, 3:-1] - row_core[:, :, 1:-3])
        - (row_core[:, :, 4:] - row_core[:, :, :-4])
    ) / 12.0

    def local_sums():
        return jnp.stack(
            [
                jnp.sum(packed_state_matrix[2] + packed_state_matrix[3]),
                jnp.sum(gradient_x[16:20] * populations),
                jnp.sum(gradient_y[16:20] * populations),
            ]
        )

    convolved, totals = convolve_and_sum(source, interaction, local_sums, primitive_tile_total)
    shielding_multiplier = 1.0 / (1.0 + SHIELDING_LEVEL * totals[0])
    self_energy = -shielding_multiplier * convolved
    section_slope = slope_terms(
        packed_state_matrix,
        energies,
        self_energy,
        gradient_x[0:16],
        gradient_y[0:16],
        dipole_x,
        dipole_y,
        driving_field,
    )
    field_next = driving_field - COUPLING * totals[1:3]
    return (section_slope, field_next)


def solution(mesh):
    in_specs = (
        P(None, "kx", "ky"),
        P(None, "kx", "ky"),
        P(None, "kx", "ky"),
        P(None, "kx", "ky"),
        P("ky", None),
        P(),
    )
    out_specs = (P(None, "kx", "ky"), P())
    return jax.shard_map(body, mesh=mesh, in_specs=in_specs, out_specs=out_specs, check_vma=False)
```

```python
import math

import jax
import numpy as np
import jax.numpy as jnp
from jax import lax
from jax.sharding import PartitionSpec as P

BAND_PAIRS = ((0, 1), (0, 2), (0, 3), (1, 2), (1, 3), (2, 3))
DEPHASING = 0.5
SHIELDING_LEVEL = 2.0
COUPLING = 40.0


def unpack(packed):
    real_entries = []
    imaginary_entries = []
    for band_one in range(4):
        real_entries.append([None, None, None, None])
        imaginary_entries.append([None, None, None, None])
    for band_one in range(4):
        real_entries[band_one][band_one] = packed[band_one]
    for number, band_pair in enumerate(BAND_PAIRS):
        upper_band, lower_band = band_pair
        real_entries[upper_band][lower_band] = packed[4 + number]
        real_entries[lower_band][upper_band] = packed[4 + number]
        imaginary_entries[upper_band][lower_band] = packed[10 + number]
        imaginary_entries[lower_band][upper_band] = -packed[10 + number]
    return (real_entries, imaginary_entries)


def product_sum(terms):
    summed = None
    for factor, left_value, right_value in terms:
        if left_value is None or right_value is None:
            continue
        product = factor * left_value * right_value
        summed = product if summed is None else summed + product
    return summed


def commutator(coupled, packed_state_matrix):
    coupled_real, coupled_imaginary = unpack(coupled)
    state_real, state_imaginary = unpack(packed_state_matrix)

    def element(row_band, column_band):
        real_terms = []
        imaginary_terms = []
        for middle in range(4):
            real_terms.append(
                (1.0, coupled_real[row_band][middle], state_real[middle][column_band])
            )
            real_terms.append(
                (-1.0, coupled_imaginary[row_band][middle], state_imaginary[middle][column_band])
            )
            real_terms.append(
                (-1.0, state_real[row_band][middle], coupled_real[middle][column_band])
            )
            real_terms.append(
                (1.0, state_imaginary[row_band][middle], coupled_imaginary[middle][column_band])
            )
            imaginary_terms.append(
                (1.0, coupled_real[row_band][middle], state_imaginary[middle][column_band])
            )
            imaginary_terms.append(
                (1.0, coupled_imaginary[row_band][middle], state_real[middle][column_band])
            )
            imaginary_terms.append(
                (-1.0, state_real[row_band][middle], coupled_imaginary[middle][column_band])
            )
            imaginary_terms.append(
                (-1.0, state_imaginary[row_band][middle], coupled_real[middle][column_band])
            )
        return (product_sum(real_terms), product_sum(imaginary_terms))

    diagonal = []
    upper_real = []
    upper_imaginary = []
    for band_one in range(4):
        diagonal.append(element(band_one, band_one)[1])
    for upper_band, lower_band in BAND_PAIRS:
        real_value, imaginary_value = element(upper_band, lower_band)
        upper_real.append(imaginary_value)
        upper_imaginary.append(-real_value)
    return jnp.stack(diagonal + upper_real + upper_imaginary)


def slope_terms(
    packed_state_matrix,
    energies,
    self_energy,
    gradient_x,
    gradient_y,
    dipole_x,
    dipole_y,
    driving_field,
):
    field_x = driving_field[0]
    field_y = driving_field[1]
    coupled = jnp.concatenate(
        [energies + self_energy[0:4], self_energy[4:16] + field_x * dipole_x + field_y * dipole_y]
    )
    rotation = commutator(coupled, packed_state_matrix)
    drift = rotation + field_x * gradient_x + field_y * gradient_y
    return jnp.concatenate([drift[0:4], drift[4:16] - DEPHASING * packed_state_matrix[4:16]])


def contract(einsum_form, left, right):
    return jnp.einsum(
        einsum_form, left, right, precision=lax.Precision.HIGHEST, preferred_element_type=jnp.float32
    )


def angles(row_count, column_count, period):
    row_index = np.arange(row_count, dtype=np.int64)[:, None]
    column_index = np.arange(column_count, dtype=np.int64)[None, :]
    return (row_index * column_index % period).astype(np.float64) * (2.0 * math.pi / period)


def table(values):
    return jnp.asarray(values.astype(np.float32))


def hartley_tables(x_length, groups, group_length):
    x_angle = angles(x_length, x_length, x_length)
    group_angle = angles(groups, groups, groups)
    twist_angle = angles(groups, group_length, groups * group_length)
    inner_angle = angles(group_length, group_length, group_length)
    return dict(
        cas_x=table(np.cos(x_angle) + np.sin(x_angle)),
        group=table(np.stack([np.cos(group_angle), -np.sin(group_angle)])),
        twist_cos=table(np.cos(twist_angle)[None, :, None, :]),
        twist_sin=table(np.sin(twist_angle)[None, :, None, :]),
        inner=table(
            np.stack(
                [np.cos(inner_angle) + np.sin(inner_angle), np.sin(inner_angle) - np.cos(inner_angle)]
            )
        ),
    )


def hartley_y(data, tables):
    first_real, first_imaginary = contract("ska,capb->sckpb", tables["group"], data)
    turned_real = first_real * tables["twist_cos"] + first_imaginary * tables["twist_sin"]
    turned_imaginary = first_imaginary * tables["twist_cos"] - first_real * tables["twist_sin"]
    turned = jnp.stack([turned_real, turned_imaginary])
    return contract("sckpb,sbq->ckpq", turned, tables["inner"])


def hartley_y_transposed(data, tables):
    turned_real, turned_imaginary = contract("ckpq,sbq->sckpb", data, tables["inner"])
    first_real = turned_real * tables["twist_cos"] - turned_imaginary * tables["twist_sin"]
    first_imaginary = turned_real * tables["twist_sin"] + turned_imaginary * tables["twist_cos"]
    first = jnp.stack([first_real, first_imaginary])
    return contract("ska,sckpb->capb", tables["group"], first)


def with_sums(data, sums, dim):
    shape = list(data.shape)
    shape[dim] = 1
    row = jnp.zeros((1, data.shape[-1]), jnp.float32).at[0, 0 : sums.shape[0]].set(sums)
    return jnp.concatenate([data, jnp.broadcast_to(row.reshape([1] * (data.ndim - 2) + [1, -1]), shape)], axis=dim)


def convolve_and_sum(source, interaction, local_sums, after_transform, primitive_tile_total):
    kx_devices = lax.axis_size("kx")
    ky_devices = lax.axis_size("ky")
    sum_count = 3
    along_kx = lax.all_to_all(source, "kx", split_axis=0, concat_axis=1, tiled=True)
    components, x_length, column_count = along_kx.shape
    row_count = x_length // ky_devices
    tables = hartley_tables(x_length, ky_devices, column_count)
    rows_x = contract("px,cxy->cpy", tables["cas_x"], along_kx)
    rows_x = after_transform(rows_x)
    split = with_sums(rows_x.reshape(components, ky_devices, row_count, column_count), local_sums(), 2)
    along_ky = lax.all_to_all(split, "ky", split_axis=1, concat_axis=1, tiled=True)
    ky_sums = jnp.sum(along_ky[0, :, row_count, 0:sum_count], axis=0)
    spectrum = hartley_y(along_ky[:, :, 0:row_count], tables)
    weight = interaction.reshape(row_count, column_count, ky_devices).transpose(2, 0, 1)
    weighted = spectrum * (weight * (1.0 / primitive_tile_total))[None]
    back_y = hartley_y_transposed(weighted, tables)
    returned = lax.all_to_all(back_y, "ky", split_axis=1, concat_axis=1, tiled=True)
    returned = returned.reshape(components, x_length, column_count)
    final = contract("px,cpy->cxy", tables["cas_x"], returned)
    rows_local = x_length // kx_devices
    final = with_sums(final.reshape(components, kx_devices, rows_local, column_count), ky_sums, 2)
    back = lax.all_to_all(final, "kx", split_axis=1, concat_axis=0, tiled=True)
    totals = jnp.sum(back[::components, 0, rows_local, 0:sum_count], axis=0) / primitive_tile_total
    convolved = back[:, 0, 0:rows_local].reshape(components * kx_devices, rows_local, column_count)
    return convolved, totals


def neighbours(array, axis, dim, width):
    devices, length = (lax.axis_size(axis), array.shape[dim])
    up = [(i, (i + 1) % devices) for i in range(devices)]
    down = [(j, i) for i, j in up]
    last = lax.slice_in_dim(array, length - width, length, axis=dim)
    initial = lax.slice_in_dim(array, 0, width, axis=dim)
    dense = (-1, 128) if last.size % 128 == 0 else last.shape
    before = lax.ppermute(last.reshape(dense), axis, up).reshape(last.shape)
    after = lax.ppermute(initial.reshape(dense), axis, down).reshape(initial.shape)
    return jnp.concatenate([before, array, after], axis=dim)


def body(packed_state_matrix, energies, dipole_x, dipole_y, interaction, driving_field):
    rows_local = packed_state_matrix.shape[1]
    columns_local = packed_state_matrix.shape[2]
    primitive_tile_total = rows_local * columns_local * lax.axis_size("kx") * lax.axis_size("ky")
    populations = packed_state_matrix[0:4]
    halo_source = []
    gradients = []

    def after_transform(rows_x):
        rows_x, late = lax.optimization_barrier((rows_x, jnp.concatenate([packed_state_matrix, energies])))
        halo_source.append(late)
        return rows_x

    def local_sums():
        column_core = neighbours(jnp.concatenate([packed_state_matrix, energies]), "kx", 1, 2)
        row_core = neighbours(halo_source[0], "ky", 2, 2)
        gradient_x = (
            8.0 * (column_core[:, 3:-1] - column_core[:, 1:-3])
            - (column_core[:, 4:] - column_core[:, :-4])
        ) / 12.0
        gradient_y = (
            8.0 * (row_core[:, :, 3:-1] - row_core[:, :, 1:-3])
            - (row_core[:, :, 4:] - row_core[:, :, :-4])
        ) / 12.0
        gradients.extend([gradient_x, gradient_y])
        return jnp.stack(
            [
                jnp.sum(packed_state_matrix[2] + packed_state_matrix[3]),
                jnp.sum(gradient_x[16:20] * populations),
                jnp.sum(gradient_y[16:20] * populations),
            ]
        )

    convolved, totals = convolve_and_sum(
        packed_state_matrix, interaction, local_sums, after_transform, primitive_tile_total
    )
    gradient_x, gradient_y = gradients
    shielding_multiplier = 1.0 / (1.0 + SHIELDING_LEVEL * totals[0])
    self_energy = -shielding_multiplier * convolved
    section_slope = slope_terms(
        packed_state_matrix,
        energies,
        self_energy,
        gradient_x[0:16],
        gradient_y[0:16],
        dipole_x,
        dipole_y,
        driving_field,
    )
    field_next = driving_field - COUPLING * totals[1:3]
    return (section_slope, field_next)


def solution(mesh):
    in_specs = (
        P(None, "kx", "ky"),
        P(None, "kx", "ky"),
        P(None, "kx", "ky"),
        P(None, "kx", "ky"),
        P("ky", None),
        P(),
    )
    out_specs = (P(None, "kx", "ky"), P())
    return jax.shard_map(body, mesh=mesh, in_specs=in_specs, out_specs=out_specs, check_vma=False)
```

```python
import math

import jax
import numpy as np
import jax.numpy as jnp
from jax import lax
from jax.sharding import PartitionSpec as P

BAND_PAIRS = ((0, 1), (0, 2), (0, 3), (1, 2), (1, 3), (2, 3))
DEPHASING = 0.5
SHIELDING_LEVEL = 2.0
COUPLING = 40.0


def unpack(packed):
    real_entries = []
    imaginary_entries = []
    for band_one in range(4):
        real_entries.append([None, None, None, None])
        imaginary_entries.append([None, None, None, None])
    for band_one in range(4):
        real_entries[band_one][band_one] = packed[band_one]
    for number, band_pair in enumerate(BAND_PAIRS):
        upper_band, lower_band = band_pair
        real_entries[upper_band][lower_band] = packed[4 + number]
        real_entries[lower_band][upper_band] = packed[4 + number]
        imaginary_entries[upper_band][lower_band] = packed[10 + number]
        imaginary_entries[lower_band][upper_band] = -packed[10 + number]
    return (real_entries, imaginary_entries)


def product_sum(terms):
    summed = None
    for factor, left_value, right_value in terms:
        if left_value is None or right_value is None:
            continue
        product = factor * left_value * right_value
        summed = product if summed is None else summed + product
    return summed


def commutator(coupled, packed_state_matrix):
    coupled_real, coupled_imaginary = unpack(coupled)
    state_real, state_imaginary = unpack(packed_state_matrix)

    def element(row_band, column_band):
        real_terms = []
        imaginary_terms = []
        for middle in range(4):
            real_terms.append(
                (1.0, coupled_real[row_band][middle], state_real[middle][column_band])
            )
            real_terms.append(
                (-1.0, coupled_imaginary[row_band][middle], state_imaginary[middle][column_band])
            )
            real_terms.append(
                (-1.0, state_real[row_band][middle], coupled_real[middle][column_band])
            )
            real_terms.append(
                (1.0, state_imaginary[row_band][middle], coupled_imaginary[middle][column_band])
            )
            imaginary_terms.append(
                (1.0, coupled_real[row_band][middle], state_imaginary[middle][column_band])
            )
            imaginary_terms.append(
                (1.0, coupled_imaginary[row_band][middle], state_real[middle][column_band])
            )
            imaginary_terms.append(
                (-1.0, state_real[row_band][middle], coupled_imaginary[middle][column_band])
            )
            imaginary_terms.append(
                (-1.0, state_imaginary[row_band][middle], coupled_real[middle][column_band])
            )
        return (product_sum(real_terms), product_sum(imaginary_terms))

    diagonal = []
    upper_real = []
    upper_imaginary = []
    for band_one in range(4):
        diagonal.append(element(band_one, band_one)[1])
    for upper_band, lower_band in BAND_PAIRS:
        real_value, imaginary_value = element(upper_band, lower_band)
        upper_real.append(imaginary_value)
        upper_imaginary.append(-real_value)
    return jnp.stack(diagonal + upper_real + upper_imaginary)


def slope_terms(
    packed_state_matrix,
    energies,
    self_energy,
    gradient_x,
    gradient_y,
    dipole_x,
    dipole_y,
    driving_field,
):
    field_x = driving_field[0]
    field_y = driving_field[1]
    coupled = jnp.concatenate(
        [energies + self_energy[0:4], self_energy[4:16] + field_x * dipole_x + field_y * dipole_y]
    )
    rotation = commutator(coupled, packed_state_matrix)
    drift = rotation + field_x * gradient_x + field_y * gradient_y
    return jnp.concatenate([drift[0:4], drift[4:16] - DEPHASING * packed_state_matrix[4:16]])


def contract(einsum_form, left, right):
    return jnp.einsum(
        einsum_form, left, right, precision=lax.Precision.HIGHEST, preferred_element_type=jnp.float32
    )


def angles(row_count, column_count, period):
    row_index = np.arange(row_count, dtype=np.int64)[:, None]
    column_index = np.arange(column_count, dtype=np.int64)[None, :]
    return (row_index * column_index % period).astype(np.float64) * (2.0 * math.pi / period)


def table(values):
    return jnp.asarray(values.astype(np.float32))


def hartley_tables(x_length, groups, group_length):
    x_angle = angles(x_length, x_length, x_length)
    group_angle = angles(groups, groups, groups)
    twist_angle = angles(groups, group_length, groups * group_length)
    inner_angle = angles(group_length, group_length, group_length)
    return dict(
        cas_x=table(np.cos(x_angle) + np.sin(x_angle)),
        group=table(np.stack([np.cos(group_angle), -np.sin(group_angle)])),
        twist_cos=table(np.cos(twist_angle)[None, :, None, :]),
        twist_sin=table(np.sin(twist_angle)[None, :, None, :]),
        inner=table(
            np.stack(
                [np.cos(inner_angle) + np.sin(inner_angle), np.sin(inner_angle) - np.cos(inner_angle)]
            )
        ),
    )


def hartley_y(data, tables):
    first_real, first_imaginary = contract("ska,capb->sckpb", tables["group"], data)
    turned_real = first_real * tables["twist_cos"] + first_imaginary * tables["twist_sin"]
    turned_imaginary = first_imaginary * tables["twist_cos"] - first_real * tables["twist_sin"]
    turned = jnp.stack([turned_real, turned_imaginary])
    return contract("sckpb,sbq->ckpq", turned, tables["inner"])


def hartley_y_transposed(data, tables):
    turned_real, turned_imaginary = contract("ckpq,sbq->sckpb", data, tables["inner"])
    first_real = turned_real * tables["twist_cos"] - turned_imaginary * tables["twist_sin"]
    first_imaginary = turned_real * tables["twist_sin"] + turned_imaginary * tables["twist_cos"]
    first = jnp.stack([first_real, first_imaginary])
    return contract("ska,sckpb->capb", tables["group"], first)


def with_sums(data, sums, dim):
    shape = list(data.shape)
    shape[dim] = 1
    row = jnp.zeros((1, data.shape[-1]), jnp.float32).at[0, 0 : sums.shape[0]].set(sums)
    return jnp.concatenate([data, jnp.broadcast_to(row.reshape([1] * (data.ndim - 2) + [1, -1]), shape)], axis=dim)


def convolve_and_sum(
    source, interaction, local_sums, after_transform, before_return, primitive_tile_total
):
    kx_devices = lax.axis_size("kx")
    ky_devices = lax.axis_size("ky")
    sum_count = 3
    along_kx = lax.all_to_all(source, "kx", split_axis=0, concat_axis=1, tiled=True)
    components, x_length, column_count = along_kx.shape
    row_count = x_length // ky_devices
    tables = hartley_tables(x_length, ky_devices, column_count)
    rows_x = contract("px,cxy->cpy", tables["cas_x"], along_kx)
    rows_x = after_transform(rows_x)
    split = rows_x.reshape(components, ky_devices, row_count, column_count)
    along_ky = lax.all_to_all(split, "ky", split_axis=1, concat_axis=1, tiled=True)
    spectrum = hartley_y(along_ky, tables)
    weight = interaction.reshape(row_count, column_count, ky_devices).transpose(2, 0, 1)
    weighted = spectrum * (weight * (1.0 / primitive_tile_total))[None]
    back_y = with_sums(hartley_y_transposed(weighted, tables), local_sums(), 2)
    returned = lax.all_to_all(back_y, "ky", split_axis=1, concat_axis=1, tiled=True)
    ky_sums = jnp.sum(returned[0, :, row_count, 0:sum_count], axis=0)
    returned = returned[:, :, 0:row_count].reshape(components, x_length, column_count)
    final = contract("px,cpy->cxy", tables["cas_x"], returned)
    rows_local = x_length // kx_devices
    final = with_sums(final.reshape(components, kx_devices, rows_local, column_count), ky_sums, 2)
    final = before_return(final)
    back = lax.all_to_all(final, "kx", split_axis=1, concat_axis=0, tiled=True)
    totals = jnp.sum(back[::components, 0, rows_local, 0:sum_count], axis=0) / primitive_tile_total
    convolved = back[:, 0, 0:rows_local].reshape(components * kx_devices, rows_local, column_count)
    return convolved, totals


def neighbours(array, axis, dim, width):
    devices, length = (lax.axis_size(axis), array.shape[dim])
    up = [(i, (i + 1) % devices) for i in range(devices)]
    down = [(j, i) for i, j in up]
    last = lax.slice_in_dim(array, length - width, length, axis=dim)
    initial = lax.slice_in_dim(array, 0, width, axis=dim)
    dense = (-1, 128) if last.size % 128 == 0 else last.shape
    before = lax.ppermute(last.reshape(dense), axis, up).reshape(last.shape)
    after = lax.ppermute(initial.reshape(dense), axis, down).reshape(initial.shape)
    return jnp.concatenate([before, array, after], axis=dim)


def body(packed_state_matrix, energies, dipole_x, dipole_y, interaction, driving_field):
    rows_local = packed_state_matrix.shape[1]
    columns_local = packed_state_matrix.shape[2]
    primitive_tile_total = rows_local * columns_local * lax.axis_size("kx") * lax.axis_size("ky")
    populations = packed_state_matrix[0:4]
    halo_source = []
    gradients = []

    def after_transform(rows_x):
        rows_x, late = lax.optimization_barrier((rows_x, jnp.concatenate([packed_state_matrix, energies])))
        halo_source.append(late)
        return rows_x

    def local_sums():
        column_core = neighbours(jnp.concatenate([packed_state_matrix, energies]), "kx", 1, 2)
        row_core = neighbours(halo_source[0], "ky", 2, 2)
        gradient_x = (
            8.0 * (column_core[:, 3:-1] - column_core[:, 1:-3])
            - (column_core[:, 4:] - column_core[:, :-4])
        ) / 12.0
        gradient_y = (
            8.0 * (row_core[:, :, 3:-1] - row_core[:, :, 1:-3])
            - (row_core[:, :, 4:] - row_core[:, :, :-4])
        ) / 12.0
        gradients.extend([gradient_x, gradient_y])
        return jnp.stack(
            [
                jnp.sum(packed_state_matrix[2] + packed_state_matrix[3]),
                jnp.sum(gradient_x[16:20] * populations),
                jnp.sum(gradient_y[16:20] * populations),
            ]
        )

    early = []

    def before_return(final):
        field_x = driving_field[0]
        field_y = driving_field[1]
        gradient_x, gradient_y = gradients
        dipole_field = field_x * dipole_x + field_y * dipole_y
        drift = field_x * gradient_x[0:16] + field_y * gradient_y[0:16]
        drift = jnp.concatenate([drift[0:4], drift[4:16] - DEPHASING * packed_state_matrix[4:16]])
        final, dipole_field, drift = lax.optimization_barrier((final, dipole_field, drift))
        early.extend([dipole_field, drift])
        return final

    convolved, totals = convolve_and_sum(
        packed_state_matrix, interaction, local_sums, after_transform, before_return, primitive_tile_total
    )
    dipole_field, drift = early
    shielding_multiplier = 1.0 / (1.0 + SHIELDING_LEVEL * totals[0])
    self_energy = -shielding_multiplier * convolved
    coupled = jnp.concatenate([energies + self_energy[0:4], self_energy[4:16] + dipole_field])
    section_slope = commutator(coupled, packed_state_matrix) + drift
    field_next = driving_field - COUPLING * totals[1:3]
    return (section_slope, field_next)


def solution(mesh):
    in_specs = (
        P(None, "kx", "ky"),
        P(None, "kx", "ky"),
        P(None, "kx", "ky"),
        P(None, "kx", "ky"),
        P("ky", None),
        P(),
    )
    out_specs = (P(None, "kx", "ky"), P())
    return jax.shard_map(body, mesh=mesh, in_specs=in_specs, out_specs=out_specs, check_vma=False)
```

```python
import math

import jax
import numpy as np
import jax.numpy as jnp
from jax import lax
from jax.sharding import PartitionSpec as P

BAND_PAIRS = ((0, 1), (0, 2), (0, 3), (1, 2), (1, 3), (2, 3))
DEPHASING = 0.5
SHIELDING_LEVEL = 2.0
COUPLING = 40.0


def unpack(packed):
    real_entries = []
    imaginary_entries = []
    for band_one in range(4):
        real_entries.append([None, None, None, None])
        imaginary_entries.append([None, None, None, None])
    for band_one in range(4):
        real_entries[band_one][band_one] = packed[band_one]
    for number, band_pair in enumerate(BAND_PAIRS):
        upper_band, lower_band = band_pair
        real_entries[upper_band][lower_band] = packed[4 + number]
        real_entries[lower_band][upper_band] = packed[4 + number]
        imaginary_entries[upper_band][lower_band] = packed[10 + number]
        imaginary_entries[lower_band][upper_band] = -packed[10 + number]
    return (real_entries, imaginary_entries)


def product_sum(terms):
    summed = None
    for factor, left_value, right_value in terms:
        if left_value is None or right_value is None:
            continue
        product = factor * left_value * right_value
        summed = product if summed is None else summed + product
    return summed


def commutator(coupled, packed_state_matrix, drift):
    coupled_real, coupled_imaginary = unpack(coupled)
    state_real, state_imaginary = unpack(packed_state_matrix)

    def element(row_band, column_band):
        real_terms = []
        imaginary_terms = []
        for middle in range(4):
            real_terms.append(
                (1.0, coupled_real[row_band][middle], state_real[middle][column_band])
            )
            real_terms.append(
                (-1.0, coupled_imaginary[row_band][middle], state_imaginary[middle][column_band])
            )
            real_terms.append(
                (-1.0, state_real[row_band][middle], coupled_real[middle][column_band])
            )
            real_terms.append(
                (1.0, state_imaginary[row_band][middle], coupled_imaginary[middle][column_band])
            )
            imaginary_terms.append(
                (1.0, coupled_real[row_band][middle], state_imaginary[middle][column_band])
            )
            imaginary_terms.append(
                (1.0, coupled_imaginary[row_band][middle], state_real[middle][column_band])
            )
            imaginary_terms.append(
                (-1.0, state_real[row_band][middle], coupled_imaginary[middle][column_band])
            )
            imaginary_terms.append(
                (-1.0, state_imaginary[row_band][middle], coupled_real[middle][column_band])
            )
        return (product_sum(real_terms), product_sum(imaginary_terms))

    diagonal = []
    upper_real = []
    upper_imaginary = []
    for band_one in range(4):
        diagonal.append(element(band_one, band_one)[1])
    for upper_band, lower_band in BAND_PAIRS:
        real_value, imaginary_value = element(upper_band, lower_band)
        upper_real.append(imaginary_value)
        upper_imaginary.append(-real_value)
    parts = diagonal + upper_real + upper_imaginary
    return jnp.stack([part + drift[number] for number, part in enumerate(parts)])


def contract(einsum_form, left, right):
    return jnp.einsum(
        einsum_form, left, right, precision=lax.Precision.HIGHEST, preferred_element_type=jnp.float32
    )


def angles(row_count, column_count, period):
    row_index = np.arange(row_count, dtype=np.int64)[:, None]
    column_index = np.arange(column_count, dtype=np.int64)[None, :]
    return (row_index * column_index % period).astype(np.float64) * (2.0 * math.pi / period)


def table(values):
    return jnp.asarray(values.astype(np.float32))


def hartley_tables(x_length, groups, group_length):
    x_angle = angles(x_length, x_length, x_length)
    group_angle = angles(groups, groups, groups)
    twist_angle = angles(groups, group_length, groups * group_length)
    inner_angle = angles(group_length, group_length, group_length)
    return dict(
        cas_x=table(np.cos(x_angle) + np.sin(x_angle)),
        group=table(np.stack([np.cos(group_angle), -np.sin(group_angle)])),
        twist_cos=table(np.cos(twist_angle)[None, :, None, :]),
        twist_sin=table(np.sin(twist_angle)[None, :, None, :]),
        inner=table(
            np.stack(
                [np.cos(inner_angle) + np.sin(inner_angle), np.sin(inner_angle) - np.cos(inner_angle)]
            )
        ),
    )


def hartley_y(data, tables):
    first_real, first_imaginary = contract("ska,capb->sckpb", tables["group"], data)
    turned_real = first_real * tables["twist_cos"] + first_imaginary * tables["twist_sin"]
    turned_imaginary = first_imaginary * tables["twist_cos"] - first_real * tables["twist_sin"]
    turned = jnp.stack([turned_real, turned_imaginary])
    return contract("sckpb,sbq->ckpq", turned, tables["inner"])


def hartley_y_transposed(data, tables):
    turned_real, turned_imaginary = contract("ckpq,sbq->sckpb", data, tables["inner"])
    first_real = turned_real * tables["twist_cos"] - turned_imaginary * tables["twist_sin"]
    first_imaginary = turned_real * tables["twist_sin"] + turned_imaginary * tables["twist_cos"]
    first = jnp.stack([first_real, first_imaginary])
    return contract("ska,sckpb->capb", tables["group"], first)


def with_sums(data, sums, dim):
    shape = list(data.shape)
    shape[dim] = 1
    row = jnp.zeros((1, data.shape[-1]), jnp.float32).at[0, 0 : sums.shape[0]].set(sums)
    return jnp.concatenate([data, jnp.broadcast_to(row.reshape([1] * (data.ndim - 2) + [1, -1]), shape)], axis=dim)


def convolve_and_sum(
    source, interaction, local_sums, after_transform, before_return, primitive_tile_total
):
    kx_devices = lax.axis_size("kx")
    ky_devices = lax.axis_size("ky")
    sum_count = 3
    along_kx = lax.all_to_all(source, "kx", split_axis=0, concat_axis=1, tiled=True)
    components, x_length, column_count = along_kx.shape
    row_count = x_length // ky_devices
    tables = hartley_tables(x_length, ky_devices, column_count)
    rows_x = contract("px,cxy->cpy", tables["cas_x"], along_kx)
    rows_x = after_transform(rows_x)
    split = rows_x.reshape(components, ky_devices, row_count, column_count)
    along_ky = lax.all_to_all(split, "ky", split_axis=1, concat_axis=1, tiled=True)
    spectrum = hartley_y(along_ky, tables)
    weight = interaction.reshape(row_count, column_count, ky_devices).transpose(2, 0, 1)
    weighted = spectrum * (weight * (1.0 / primitive_tile_total))[None]
    back_y = with_sums(hartley_y_transposed(weighted, tables), local_sums(), 2)
    returned = lax.all_to_all(back_y, "ky", split_axis=1, concat_axis=1, tiled=True)
    ky_sums = jnp.sum(returned[0, :, row_count, 0:sum_count], axis=0)
    returned = returned[:, :, 0:row_count].reshape(components, x_length, column_count)
    final = contract("px,cpy->cxy", tables["cas_x"], returned)
    rows_local = x_length // kx_devices
    final = with_sums(final.reshape(components, kx_devices, rows_local, column_count), ky_sums, 2)
    final = before_return(final)
    back = lax.all_to_all(final, "kx", split_axis=1, concat_axis=0, tiled=True)
    totals = jnp.sum(back[::components, 0, rows_local, 0:sum_count], axis=0) / primitive_tile_total
    convolved = back[:, 0, 0:rows_local].reshape(components * kx_devices, rows_local, column_count)
    return convolved, totals


def neighbours(array, axis, dim, width):
    devices, length = (lax.axis_size(axis), array.shape[dim])
    up = [(i, (i + 1) % devices) for i in range(devices)]
    down = [(j, i) for i, j in up]
    last = lax.slice_in_dim(array, length - width, length, axis=dim)
    initial = lax.slice_in_dim(array, 0, width, axis=dim)
    dense = (-1, 128) if last.size % 128 == 0 else last.shape
    before = lax.ppermute(last.reshape(dense), axis, up).reshape(last.shape)
    after = lax.ppermute(initial.reshape(dense), axis, down).reshape(initial.shape)
    return jnp.concatenate([before, array, after], axis=dim)


def body(packed_state_matrix, energies, dipole_x, dipole_y, interaction, driving_field):
    rows_local = packed_state_matrix.shape[1]
    columns_local = packed_state_matrix.shape[2]
    primitive_tile_total = rows_local * columns_local * lax.axis_size("kx") * lax.axis_size("ky")
    populations = packed_state_matrix[0:4]
    halo_source = []
    gradients = []

    def after_transform(rows_x):
        rows_x, late = lax.optimization_barrier((rows_x, jnp.concatenate([packed_state_matrix, energies])))
        halo_source.append(late)
        return rows_x

    def local_sums():
        column_core = neighbours(jnp.concatenate([packed_state_matrix, energies]), "kx", 1, 2)
        row_core = neighbours(halo_source[0], "ky", 2, 2)
        gradient_x = (
            8.0 * (column_core[:, 3:-1] - column_core[:, 1:-3])
            - (column_core[:, 4:] - column_core[:, :-4])
        ) / 12.0
        gradient_y = (
            8.0 * (row_core[:, :, 3:-1] - row_core[:, :, 1:-3])
            - (row_core[:, :, 4:] - row_core[:, :, :-4])
        ) / 12.0
        gradients.extend([gradient_x, gradient_y])
        return jnp.stack(
            [
                jnp.sum(packed_state_matrix[2] + packed_state_matrix[3]),
                jnp.sum(gradient_x[16:20] * populations),
                jnp.sum(gradient_y[16:20] * populations),
            ]
        )

    early = []

    def before_return(final):
        field_x = driving_field[0]
        field_y = driving_field[1]
        gradient_x, gradient_y = gradients
        dipole_field = field_x * dipole_x + field_y * dipole_y
        drift = field_x * gradient_x[0:16] + field_y * gradient_y[0:16]
        drift = jnp.concatenate([drift[0:4], drift[4:16] - DEPHASING * packed_state_matrix[4:16]])
        final, dipole_field, drift = lax.optimization_barrier((final, dipole_field, drift))
        early.extend([dipole_field, drift])
        return final

    convolved, totals = convolve_and_sum(
        packed_state_matrix, interaction, local_sums, after_transform, before_return, primitive_tile_total
    )
    dipole_field, drift = early
    shielding_multiplier = 1.0 / (1.0 + SHIELDING_LEVEL * totals[0])
    self_energy = -shielding_multiplier * convolved
    coupled = jnp.concatenate([energies + self_energy[0:4], self_energy[4:16] + dipole_field])
    section_slope = commutator(coupled, packed_state_matrix, drift)
    field_next = driving_field - COUPLING * totals[1:3]
    return (section_slope, field_next)


def solution(mesh):
    in_specs = (
        P(None, "kx", "ky"),
        P(None, "kx", "ky"),
        P(None, "kx", "ky"),
        P(None, "kx", "ky"),
        P("ky", None),
        P(),
    )
    out_specs = (P(None, "kx", "ky"), P())
    return jax.shard_map(body, mesh=mesh, in_specs=in_specs, out_specs=out_specs, check_vma=False)
```

```python
import math

import jax
import numpy as np
import jax.numpy as jnp
from jax import lax
from jax.sharding import PartitionSpec as P

BAND_PAIRS = ((0, 1), (0, 2), (0, 3), (1, 2), (1, 3), (2, 3))
DEPHASING = 0.5
SHIELDING_LEVEL = 2.0
COUPLING = 40.0


def unpack(packed):
    real_entries = []
    imaginary_entries = []
    for band_one in range(4):
        real_entries.append([None, None, None, None])
        imaginary_entries.append([None, None, None, None])
    for band_one in range(4):
        real_entries[band_one][band_one] = packed[band_one]
    for number, band_pair in enumerate(BAND_PAIRS):
        upper_band, lower_band = band_pair
        real_entries[upper_band][lower_band] = packed[4 + number]
        real_entries[lower_band][upper_band] = packed[4 + number]
        imaginary_entries[upper_band][lower_band] = packed[10 + number]
        imaginary_entries[lower_band][upper_band] = -packed[10 + number]
    return (real_entries, imaginary_entries)


def product_sum(terms):
    summed = None
    for factor, left_value, right_value in terms:
        if left_value is None or right_value is None:
            continue
        product = factor * left_value * right_value
        summed = product if summed is None else summed + product
    return summed


def commutator(coupled, packed_state_matrix):
    coupled_real, coupled_imaginary = unpack(coupled)
    state_real, state_imaginary = unpack(packed_state_matrix)

    def element(row_band, column_band):
        real_terms = []
        imaginary_terms = []
        for middle in range(4):
            real_terms.append(
                (1.0, coupled_real[row_band][middle], state_real[middle][column_band])
            )
            real_terms.append(
                (-1.0, coupled_imaginary[row_band][middle], state_imaginary[middle][column_band])
            )
            real_terms.append(
                (-1.0, state_real[row_band][middle], coupled_real[middle][column_band])
            )
            real_terms.append(
                (1.0, state_imaginary[row_band][middle], coupled_imaginary[middle][column_band])
            )
            imaginary_terms.append(
                (1.0, coupled_real[row_band][middle], state_imaginary[middle][column_band])
            )
            imaginary_terms.append(
                (1.0, coupled_imaginary[row_band][middle], state_real[middle][column_band])
            )
            imaginary_terms.append(
                (-1.0, state_real[row_band][middle], coupled_imaginary[middle][column_band])
            )
            imaginary_terms.append(
                (-1.0, state_imaginary[row_band][middle], coupled_real[middle][column_band])
            )
        return (product_sum(real_terms), product_sum(imaginary_terms))

    diagonal = []
    upper_real = []
    upper_imaginary = []
    for band_one in range(4):
        diagonal.append(element(band_one, band_one)[1])
    for upper_band, lower_band in BAND_PAIRS:
        real_value, imaginary_value = element(upper_band, lower_band)
        upper_real.append(imaginary_value)
        upper_imaginary.append(-real_value)
    return jnp.stack(diagonal + upper_real + upper_imaginary)


def slope_terms(
    packed_state_matrix,
    energies,
    self_energy,
    gradient_x,
    gradient_y,
    dipole_x,
    dipole_y,
    driving_field,
):
    field_x = driving_field[0]
    field_y = driving_field[1]
    coupled = jnp.concatenate(
        [energies + self_energy[0:4], self_energy[4:16] + field_x * dipole_x + field_y * dipole_y]
    )
    rotation = commutator(coupled, packed_state_matrix)
    drift = rotation + field_x * gradient_x + field_y * gradient_y
    return jnp.concatenate([drift[0:4], drift[4:16] - DEPHASING * packed_state_matrix[4:16]])


def contract(einsum_form, left, right):
    return jnp.einsum(
        einsum_form, left, right, precision=lax.Precision.HIGHEST, preferred_element_type=jnp.float32
    )


def angles(row_count, column_count, period):
    row_index = np.arange(row_count, dtype=np.int64)[:, None]
    column_index = np.arange(column_count, dtype=np.int64)[None, :]
    return (row_index * column_index % period).astype(np.float64) * (2.0 * math.pi / period)


def table(values):
    return jnp.asarray(values.astype(np.float32))


def hartley_tables(x_length, groups, group_length):
    x_angle = angles(x_length, x_length, x_length)
    group_angle = angles(groups, groups, groups)
    twist_angle = angles(groups, group_length, groups * group_length)
    inner_angle = angles(group_length, group_length, group_length)
    return dict(
        cas_x=table(np.cos(x_angle) + np.sin(x_angle)),
        group=table(np.stack([np.cos(group_angle), -np.sin(group_angle)])),
        twist_cos=table(np.cos(twist_angle)[None, :, None, :]),
        twist_sin=table(np.sin(twist_angle)[None, :, None, :]),
        inner=table(
            np.stack(
                [np.cos(inner_angle) + np.sin(inner_angle), np.sin(inner_angle) - np.cos(inner_angle)]
            )
        ),
    )


def hartley_y(data, tables):
    first_real, first_imaginary = contract("ska,capb->sckpb", tables["group"], data)
    turned_real = first_real * tables["twist_cos"] + first_imaginary * tables["twist_sin"]
    turned_imaginary = first_imaginary * tables["twist_cos"] - first_real * tables["twist_sin"]
    turned = jnp.stack([turned_real, turned_imaginary])
    return contract("sckpb,sbq->ckpq", turned, tables["inner"])


def hartley_y_transposed(data, tables):
    turned_real, turned_imaginary = contract("ckpq,sbq->sckpb", data, tables["inner"])
    first_real = turned_real * tables["twist_cos"] - turned_imaginary * tables["twist_sin"]
    first_imaginary = turned_real * tables["twist_sin"] + turned_imaginary * tables["twist_cos"]
    first = jnp.stack([first_real, first_imaginary])
    return contract("ska,sckpb->capb", tables["group"], first)


def with_sums(data, sums, dim):
    shape = list(data.shape)
    shape[dim] = 1
    row = jnp.zeros((1, data.shape[-1]), jnp.float32).at[0, 0 : sums.shape[0]].set(sums)
    return jnp.concatenate([data, jnp.broadcast_to(row.reshape([1] * (data.ndim - 2) + [1, -1]), shape)], axis=dim)


def convolve_and_sum(
    source, interaction, local_sums, after_transform, before_return, primitive_tile_total
):
    kx_devices = lax.axis_size("kx")
    ky_devices = lax.axis_size("ky")
    sum_count = 3
    along_kx = lax.all_to_all(source, "kx", split_axis=0, concat_axis=1, tiled=True)
    components, x_length, column_count = along_kx.shape
    row_count = x_length // ky_devices
    tables = hartley_tables(x_length, ky_devices, column_count)
    rows_x = contract("px,cxy->cpy", tables["cas_x"], along_kx)
    rows_x = after_transform(rows_x)
    split = rows_x.reshape(components, ky_devices, row_count, column_count)
    along_ky = lax.all_to_all(split, "ky", split_axis=1, concat_axis=1, tiled=True)
    spectrum = hartley_y(along_ky, tables)
    weight = interaction.reshape(row_count, column_count, ky_devices).transpose(2, 0, 1)
    weighted = spectrum * (weight * (1.0 / primitive_tile_total))[None]
    back_y = with_sums(hartley_y_transposed(weighted, tables), local_sums(), 2)
    returned = before_return(lax.all_to_all(back_y, "ky", split_axis=1, concat_axis=1, tiled=True))
    ky_sums = jnp.sum(returned[0, :, row_count, 0:sum_count], axis=0)
    returned = returned[:, :, 0:row_count].reshape(components, x_length, column_count)
    final = contract("px,cpy->cxy", tables["cas_x"], returned)
    rows_local = x_length // kx_devices
    final = with_sums(final.reshape(components, kx_devices, rows_local, column_count), ky_sums, 2)
    back = lax.all_to_all(final, "kx", split_axis=1, concat_axis=0, tiled=True)
    totals = jnp.sum(back[::components, 0, rows_local, 0:sum_count], axis=0) / primitive_tile_total
    convolved = back[:, 0, 0:rows_local].reshape(components * kx_devices, rows_local, column_count)
    return convolved, totals


def neighbours(array, axis, dim, width):
    devices, length = (lax.axis_size(axis), array.shape[dim])
    up = [(i, (i + 1) % devices) for i in range(devices)]
    down = [(j, i) for i, j in up]
    last = lax.slice_in_dim(array, length - width, length, axis=dim)
    initial = lax.slice_in_dim(array, 0, width, axis=dim)
    dense = (-1, 128) if last.size % 128 == 0 else last.shape
    before = lax.ppermute(last.reshape(dense), axis, up).reshape(last.shape)
    after = lax.ppermute(initial.reshape(dense), axis, down).reshape(initial.shape)
    return jnp.concatenate([before, array, after], axis=dim)


def body(packed_state_matrix, energies, dipole_x, dipole_y, interaction, driving_field):
    rows_local = packed_state_matrix.shape[1]
    columns_local = packed_state_matrix.shape[2]
    primitive_tile_total = rows_local * columns_local * lax.axis_size("kx") * lax.axis_size("ky")
    populations = packed_state_matrix[0:4]
    halo_source = []
    gradients = []

    def after_transform(rows_x):
        rows_x, late = lax.optimization_barrier((rows_x, jnp.concatenate([packed_state_matrix, energies])))
        halo_source.append(late)
        return rows_x

    def local_sums():
        column_core = neighbours(jnp.concatenate([packed_state_matrix, energies]), "kx", 1, 2)
        row_core = neighbours(halo_source[0], "ky", 2, 2)
        gradient_x = (
            8.0 * (column_core[:, 3:-1] - column_core[:, 1:-3])
            - (column_core[:, 4:] - column_core[:, :-4])
        ) / 12.0
        gradient_y = (
            8.0 * (row_core[:, :, 3:-1] - row_core[:, :, 1:-3])
            - (row_core[:, :, 4:] - row_core[:, :, :-4])
        ) / 12.0
        gradients.extend([gradient_x, gradient_y])
        return jnp.stack(
            [
                jnp.sum(packed_state_matrix[2] + packed_state_matrix[3]),
                jnp.sum(gradient_x[16:20] * populations),
                jnp.sum(gradient_y[16:20] * populations),
            ]
        )

    early = []

    def before_return(final):
        field_x = driving_field[0]
        field_y = driving_field[1]
        gradient_x, gradient_y = gradients
        dipole_field = field_x * dipole_x + field_y * dipole_y
        drift = field_x * gradient_x[0:16] + field_y * gradient_y[0:16]
        drift = jnp.concatenate([drift[0:4], drift[4:16] - DEPHASING * packed_state_matrix[4:16]])
        final, dipole_field, drift = lax.optimization_barrier((final, dipole_field, drift))
        early.extend([dipole_field, drift])
        return final

    convolved, totals = convolve_and_sum(
        packed_state_matrix, interaction, local_sums, after_transform, before_return, primitive_tile_total
    )
    dipole_field, drift = early
    shielding_multiplier = 1.0 / (1.0 + SHIELDING_LEVEL * totals[0])
    self_energy = -shielding_multiplier * convolved
    coupled = jnp.concatenate([energies + self_energy[0:4], self_energy[4:16] + dipole_field])
    section_slope = commutator(coupled, packed_state_matrix) + drift
    field_next = driving_field - COUPLING * totals[1:3]
    return (section_slope, field_next)


def solution(mesh):
    in_specs = (
        P(None, "kx", "ky"),
        P(None, "kx", "ky"),
        P(None, "kx", "ky"),
        P(None, "kx", "ky"),
        P("ky", None),
        P(),
    )
    out_specs = (P(None, "kx", "ky"), P())
    return jax.shard_map(body, mesh=mesh, in_specs=in_specs, out_specs=out_specs, check_vma=False)
```

```python
import math

import jax
import numpy as np
import jax.numpy as jnp
from jax import lax
from jax.sharding import PartitionSpec as P

BAND_PAIRS = ((0, 1), (0, 2), (0, 3), (1, 2), (1, 3), (2, 3))
DEPHASING = 0.5
SHIELDING_LEVEL = 2.0
COUPLING = 40.0


def unpack(packed):
    real_entries = []
    imaginary_entries = []
    for band_one in range(4):
        real_entries.append([None, None, None, None])
        imaginary_entries.append([None, None, None, None])
    for band_one in range(4):
        real_entries[band_one][band_one] = packed[band_one]
    for number, band_pair in enumerate(BAND_PAIRS):
        upper_band, lower_band = band_pair
        real_entries[upper_band][lower_band] = packed[4 + number]
        real_entries[lower_band][upper_band] = packed[4 + number]
        imaginary_entries[upper_band][lower_band] = packed[10 + number]
        imaginary_entries[lower_band][upper_band] = -packed[10 + number]
    return (real_entries, imaginary_entries)


def product_sum(terms):
    summed = None
    for factor, left_value, right_value in terms:
        if left_value is None or right_value is None:
            continue
        product = factor * left_value * right_value
        summed = product if summed is None else summed + product
    return summed


def commutator(coupled, packed_state_matrix):
    coupled_real, coupled_imaginary = unpack(coupled)
    state_real, state_imaginary = unpack(packed_state_matrix)

    def element(row_band, column_band):
        real_terms = []
        imaginary_terms = []
        for middle in range(4):
            real_terms.append(
                (1.0, coupled_real[row_band][middle], state_real[middle][column_band])
            )
            real_terms.append(
                (-1.0, coupled_imaginary[row_band][middle], state_imaginary[middle][column_band])
            )
            real_terms.append(
                (-1.0, state_real[row_band][middle], coupled_real[middle][column_band])
            )
            real_terms.append(
                (1.0, state_imaginary[row_band][middle], coupled_imaginary[middle][column_band])
            )
            imaginary_terms.append(
                (1.0, coupled_real[row_band][middle], state_imaginary[middle][column_band])
            )
            imaginary_terms.append(
                (1.0, coupled_imaginary[row_band][middle], state_real[middle][column_band])
            )
            imaginary_terms.append(
                (-1.0, state_real[row_band][middle], coupled_imaginary[middle][column_band])
            )
            imaginary_terms.append(
                (-1.0, state_imaginary[row_band][middle], coupled_real[middle][column_band])
            )
        return (product_sum(real_terms), product_sum(imaginary_terms))

    diagonal = []
    upper_real = []
    upper_imaginary = []
    for band_one in range(4):
        diagonal.append(element(band_one, band_one)[1])
    for upper_band, lower_band in BAND_PAIRS:
        real_value, imaginary_value = element(upper_band, lower_band)
        upper_real.append(imaginary_value)
        upper_imaginary.append(-real_value)
    return jnp.stack(diagonal + upper_real + upper_imaginary)


def slope_terms(
    packed_state_matrix,
    energies,
    self_energy,
    gradient_x,
    gradient_y,
    dipole_x,
    dipole_y,
    driving_field,
):
    field_x = driving_field[0]
    field_y = driving_field[1]
    coupled = jnp.concatenate(
        [energies + self_energy[0:4], self_energy[4:16] + field_x * dipole_x + field_y * dipole_y]
    )
    rotation = commutator(coupled, packed_state_matrix)
    drift = rotation + field_x * gradient_x + field_y * gradient_y
    return jnp.concatenate([drift[0:4], drift[4:16] - DEPHASING * packed_state_matrix[4:16]])


def contract(einsum_form, left, right):
    return jnp.einsum(
        einsum_form, left, right, precision=lax.Precision.HIGH, preferred_element_type=jnp.float32
    )


def angles(row_count, column_count, period):
    row_index = np.arange(row_count, dtype=np.int64)[:, None]
    column_index = np.arange(column_count, dtype=np.int64)[None, :]
    return (row_index * column_index % period).astype(np.float64) * (2.0 * math.pi / period)


def table(values):
    return jnp.asarray(values.astype(np.float32))


def hartley_tables(x_length, groups, group_length):
    x_angle = angles(x_length, x_length, x_length)
    group_angle = angles(groups, groups, groups)
    twist_angle = angles(groups, group_length, groups * group_length)
    inner_angle = angles(group_length, group_length, group_length)
    return dict(
        cas_x=table(np.cos(x_angle) + np.sin(x_angle)),
        group=table(np.stack([np.cos(group_angle), -np.sin(group_angle)])),
        twist_cos=table(np.cos(twist_angle)[None, :, None, :]),
        twist_sin=table(np.sin(twist_angle)[None, :, None, :]),
        inner=table(
            np.stack(
                [np.cos(inner_angle) + np.sin(inner_angle), np.sin(inner_angle) - np.cos(inner_angle)]
            )
        ),
    )


def hartley_y(data, tables):
    first_real, first_imaginary = contract("ska,capb->sckpb", tables["group"], data)
    turned_real = first_real * tables["twist_cos"] + first_imaginary * tables["twist_sin"]
    turned_imaginary = first_imaginary * tables["twist_cos"] - first_real * tables["twist_sin"]
    turned = jnp.stack([turned_real, turned_imaginary])
    return contract("sckpb,sbq->ckpq", turned, tables["inner"])


def hartley_y_transposed(data, tables):
    turned_real, turned_imaginary = contract("ckpq,sbq->sckpb", data, tables["inner"])
    first_real = turned_real * tables["twist_cos"] - turned_imaginary * tables["twist_sin"]
    first_imaginary = turned_real * tables["twist_sin"] + turned_imaginary * tables["twist_cos"]
    first = jnp.stack([first_real, first_imaginary])
    return contract("ska,sckpb->capb", tables["group"], first)


def with_sums(data, sums, dim):
    shape = list(data.shape)
    shape[dim] = 1
    row = jnp.zeros((1, data.shape[-1]), jnp.float32).at[0, 0 : sums.shape[0]].set(sums)
    return jnp.concatenate([data, jnp.broadcast_to(row.reshape([1] * (data.ndim - 2) + [1, -1]), shape)], axis=dim)


def convolve_and_sum(
    source, interaction, local_sums, after_transform, before_return, primitive_tile_total
):
    kx_devices = lax.axis_size("kx")
    ky_devices = lax.axis_size("ky")
    sum_count = 3
    along_kx = lax.all_to_all(source, "kx", split_axis=0, concat_axis=1, tiled=True)
    components, x_length, column_count = along_kx.shape
    row_count = x_length // ky_devices
    tables = hartley_tables(x_length, ky_devices, column_count)
    rows_x = contract("px,cxy->cpy", tables["cas_x"], along_kx)
    rows_x = after_transform(rows_x)
    split = rows_x.reshape(components, ky_devices, row_count, column_count)
    along_ky = lax.all_to_all(split, "ky", split_axis=1, concat_axis=1, tiled=True)
    spectrum = hartley_y(along_ky, tables)
    weight = interaction.reshape(row_count, column_count, ky_devices).transpose(2, 0, 1)
    weighted = spectrum * (weight * (1.0 / primitive_tile_total))[None]
    back_y = with_sums(hartley_y_transposed(weighted, tables), local_sums(), 2)
    returned = before_return(lax.all_to_all(back_y, "ky", split_axis=1, concat_axis=1, tiled=True))
    ky_sums = jnp.sum(returned[0, :, row_count, 0:sum_count], axis=0)
    returned = returned[:, :, 0:row_count].reshape(components, x_length, column_count)
    final = contract("px,cpy->cxy", tables["cas_x"], returned)
    rows_local = x_length // kx_devices
    final = with_sums(final.reshape(components, kx_devices, rows_local, column_count), ky_sums, 2)
    back = lax.all_to_all(final, "kx", split_axis=1, concat_axis=0, tiled=True)
    totals = jnp.sum(back[::components, 0, rows_local, 0:sum_count], axis=0) / primitive_tile_total
    convolved = back[:, 0, 0:rows_local].reshape(components * kx_devices, rows_local, column_count)
    return convolved, totals


def neighbours(array, axis, dim, width):
    devices, length = (lax.axis_size(axis), array.shape[dim])
    up = [(i, (i + 1) % devices) for i in range(devices)]
    down = [(j, i) for i, j in up]
    last = lax.slice_in_dim(array, length - width, length, axis=dim)
    initial = lax.slice_in_dim(array, 0, width, axis=dim)
    dense = (-1, 128) if last.size % 128 == 0 else last.shape
    before = lax.ppermute(last.reshape(dense), axis, up).reshape(last.shape)
    after = lax.ppermute(initial.reshape(dense), axis, down).reshape(initial.shape)
    return jnp.concatenate([before, array, after], axis=dim)


def body(packed_state_matrix, energies, dipole_x, dipole_y, interaction, driving_field):
    rows_local = packed_state_matrix.shape[1]
    columns_local = packed_state_matrix.shape[2]
    primitive_tile_total = rows_local * columns_local * lax.axis_size("kx") * lax.axis_size("ky")
    populations = packed_state_matrix[0:4]
    halo_source = []
    gradients = []

    def after_transform(rows_x):
        rows_x, late = lax.optimization_barrier((rows_x, jnp.concatenate([packed_state_matrix, energies])))
        halo_source.append(late)
        return rows_x

    def local_sums():
        column_core = neighbours(jnp.concatenate([packed_state_matrix, energies]), "kx", 1, 2)
        row_core = neighbours(halo_source[0], "ky", 2, 2)
        gradient_x = (
            8.0 * (column_core[:, 3:-1] - column_core[:, 1:-3])
            - (column_core[:, 4:] - column_core[:, :-4])
        ) / 12.0
        gradient_y = (
            8.0 * (row_core[:, :, 3:-1] - row_core[:, :, 1:-3])
            - (row_core[:, :, 4:] - row_core[:, :, :-4])
        ) / 12.0
        gradients.extend([gradient_x, gradient_y])
        return jnp.stack(
            [
                jnp.sum(packed_state_matrix[2] + packed_state_matrix[3]),
                jnp.sum(gradient_x[16:20] * populations),
                jnp.sum(gradient_y[16:20] * populations),
            ]
        )

    early = []

    def before_return(final):
        field_x = driving_field[0]
        field_y = driving_field[1]
        gradient_x, gradient_y = gradients
        dipole_field = field_x * dipole_x + field_y * dipole_y
        drift = field_x * gradient_x[0:16] + field_y * gradient_y[0:16]
        drift = jnp.concatenate([drift[0:4], drift[4:16] - DEPHASING * packed_state_matrix[4:16]])
        final, dipole_field, drift = lax.optimization_barrier((final, dipole_field, drift))
        early.extend([dipole_field, drift])
        return final

    convolved, totals = convolve_and_sum(
        packed_state_matrix, interaction, local_sums, after_transform, before_return, primitive_tile_total
    )
    dipole_field, drift = early
    shielding_multiplier = 1.0 / (1.0 + SHIELDING_LEVEL * totals[0])
    self_energy = -shielding_multiplier * convolved
    coupled = jnp.concatenate([energies + self_energy[0:4], self_energy[4:16] + dipole_field])
    section_slope = commutator(coupled, packed_state_matrix) + drift
    field_next = driving_field - COUPLING * totals[1:3]
    return (section_slope, field_next)


def solution(mesh):
    in_specs = (
        P(None, "kx", "ky"),
        P(None, "kx", "ky"),
        P(None, "kx", "ky"),
        P(None, "kx", "ky"),
        P("ky", None),
        P(),
    )
    out_specs = (P(None, "kx", "ky"), P())
    return jax.shard_map(body, mesh=mesh, in_specs=in_specs, out_specs=out_specs, check_vma=False)
```
